512 devices in a mesh: prompt: 32 (over x, y), sample: 16 (over z, core).
Axes of the slice: x: 4, y: 8, z: 8, core: 2. Of those that a mesh axis runs over, the one named last changes fastest.
Arguments:
- queries: bfloat16 [32, 16, 4, 8192], P('prompt', 'sample'), may hold values from -24 to 24
- new_kv: bfloat16 [32, 16, 4, 2, 1024], P('prompt', 'sample'), may hold values from -24 to 24
- suffix_kv: bfloat16 [32, 16, 256, 2, 1024], P('prompt', 'sample'), may hold values from -24 to 24
- suffix_len: int32 [32, 16], P('prompt', 'sample'), may hold values from 1 to 256, as said below
- prefix_head: bfloat16 [32, 2048, 2, 1024], P('prompt', 'sample'), may hold values from -24 to 24
- prefix_tail: bfloat16 [32, 2048, 2, 1024], P('prompt', 'sample'), may hold values from -24 to 24
- prefix_len: int32 [32], replicated, may hold values from 1024 to 4096, as said below
Outputs:
- attended: bfloat16 [32, 16, 4, 8192], P('prompt', 'sample')
The draws below stay inside these ranges and needn't reach their ends.
Inputs may be any that keep to these rules, and one draw needn't show every extreme that they name: `suffix_len`: some sample has all 256 slots live and some only one. `prefix_len`: some prompt has all 4096 positions live and some only 1024.
All inputs are finite; a program needn't handle non-finite values.
Results may differ from the reference program's by a relative error of at most 0.001.
Values may be sent and summed in bfloat16 or wider, within the bound.
No kernel may reach another device: no remote copies, remote signals or barrier semaphores. Data moves between devices by JAX's collectives and lax.ppermute only.
A program may use at most 64 MiB of HBM per device.

```python
import jax
import jax.numpy as jnp
from jax import lax

QH = 64
KVH = 8
HEAD_SIZE = 128
SUF = 256
STEPS = 4
PROMPTS = 32
SAMPLES = 16
HALF = 2048
PREFIX = 4096


def kv_pairs(key, dims_shape):
    sample_base = jnp.clip(jax.random.normal(key, dims_shape, jnp.float32), -6.0, 6.0)
    scales = jnp.array([1.0, 4.0], jnp.float32).reshape(2, 1)
    return sample_base * scales


def draw_queries(key, part):
    own_key = jax.random.fold_in(key, 12)
    dims_shape = (PROMPTS, SAMPLES, STEPS, QH, HEAD_SIZE)
    sample_base = 2.0 * jnp.clip(jax.random.normal(own_key, dims_shape, jnp.float32), -6.0, 6.0)
    return sample_base.reshape(PROMPTS, SAMPLES, STEPS, QH * HEAD_SIZE).astype(jnp.bfloat16)


def draw_new_kv(key, part):
    return kv_pairs(jax.random.fold_in(key, 13), (PROMPTS, SAMPLES, STEPS, 2, KVH * HEAD_SIZE)).astype(jnp.bfloat16)


def draw_suffix_kv(key, part):
    return kv_pairs(jax.random.fold_in(key, 14), (PROMPTS, SAMPLES, SUF, 2, KVH * HEAD_SIZE)).astype(jnp.bfloat16)


def draw_prefix_head(key, part):
    sample_base = kv_pairs(jax.random.fold_in(key, 15), (PROMPTS, HALF, 2, KVH * HEAD_SIZE))
    return sample_base.astype(jnp.bfloat16)


def draw_prefix_tail(key, part):
    return kv_pairs(jax.random.fold_in(key, 16), (PROMPTS, HALF, 2, KVH * HEAD_SIZE)).astype(jnp.bfloat16)


def draw_suffix_len(key, part):
    own_key = jax.random.fold_in(key, 17)
    lengths = jax.random.randint(own_key, (PROMPTS * SAMPLES,), 1, SUF + 1)
    first = jax.random.randint(jax.random.fold_in(own_key, 1), (), 0, PROMPTS * SAMPLES)
    second = (first + 1 + jax.random.randint(jax.random.fold_in(own_key, 2), (), 0, PROMPTS * SAMPLES - 1)) % (PROMPTS * SAMPLES)
    lengths = lengths.at[first].set(SUF)
    lengths = lengths.at[second].set(1)
    return lengths.reshape(PROMPTS, SAMPLES).astype(jnp.int32)


def draw_prefix_len(key, part):
    own_key = jax.random.fold_in(key, 18)
    lengths = jax.random.randint(own_key, (PROMPTS,), PREFIX // 4, PREFIX + 1)
    first = jax.random.randint(jax.random.fold_in(own_key, 1), (), 0, PROMPTS)
    second = (first + 1) % PROMPTS
    lengths = lengths.at[first].set(PREFIX)
    lengths = lengths.at[second].set(PREFIX // 4)
    return lengths.astype(jnp.int32)


def setup_inputs(seed: int = 0) -> dict:
    arg_keys = jax.random.split(jax.random.key(seed), 8)
    return {
        "queries": draw_queries(jax.random.fold_in(arg_keys[7], 71), 0),
        "new_kv": draw_new_kv(jax.random.fold_in(arg_keys[7], 71), 0),
        "suffix_kv": draw_suffix_kv(jax.random.fold_in(arg_keys[7], 71), 0),
        "suffix_len": draw_suffix_len(jax.random.fold_in(arg_keys[7], 71), 0),
        "prefix_head": draw_prefix_head(jax.random.fold_in(arg_keys[7], 71), 0),
        "prefix_tail": draw_prefix_tail(jax.random.fold_in(arg_keys[7], 71), 0),
        "prefix_len": draw_prefix_len(jax.random.fold_in(arg_keys[7], 71), 0),
    }


NEG = -1e30


def apply_weights(logit_scores, valid_mask, value_matrix, form):
    masked = jnp.where(valid_mask, logit_scores, NEG)
    maxima = jnp.max(masked, axis=-1)
    weights = jnp.where(valid_mask, jnp.exp(masked - maxima[..., None]), 0.0)
    totals = jnp.sum(weights, axis=-1)
    numerator = jnp.einsum(form, weights, value_matrix, precision=lax.Precision.HIGHEST)
    leading = numerator.shape[:2]
    return (numerator.reshape(leading + (QH, HEAD_SIZE)), maxima.reshape(leading + (QH,)), totals.reshape(leading + (QH,)))


def prefix_terms(query_rows, pairs, start, length):
    sample_count, step_count = query_rows.shape[0], query_rows.shape[1]
    block_len = pairs.shape[0]
    grouped_queries = query_rows.reshape(sample_count, step_count, KVH, QH // KVH, HEAD_SIZE).astype(jnp.float32)
    key_matrix = pairs[:, 0].reshape(block_len, KVH, HEAD_SIZE).astype(jnp.float32)
    value_matrix = pairs[:, 1].reshape(block_len, KVH, HEAD_SIZE).astype(jnp.float32)
    logit_scores = jnp.einsum("rhlxf,vlf->rhlxv", grouped_queries, key_matrix, precision=lax.Precision.HIGHEST) * (HEAD_SIZE ** -0.5)
    valid_mask = (start + jnp.arange(block_len, dtype=jnp.int32)) < length
    return apply_weights(logit_scores, valid_mask, value_matrix, "urpyj,jpi->urpyi")


def suffix_terms(query_rows, cache, fresh, length):
    sample_count, step_count = query_rows.shape[0], query_rows.shape[1]
    slots = cache.shape[1]
    joined = jnp.concatenate([cache, fresh], axis=1)
    total_len = joined.shape[1]
    grouped_queries = query_rows.reshape(sample_count, step_count, KVH, QH // KVH, HEAD_SIZE).astype(jnp.float32)
    key_matrix = joined[:, :, 0].reshape(sample_count, total_len, KVH, HEAD_SIZE).astype(jnp.float32)
    value_matrix = joined[:, :, 1].reshape(sample_count, total_len, KVH, HEAD_SIZE).astype(jnp.float32)
    logit_scores = jnp.einsum("stkgd,slkd->stkgl", grouped_queries, key_matrix, precision=lax.Precision.HIGHEST) * (HEAD_SIZE ** -0.5)
    cache_live = jnp.arange(slots, dtype=jnp.int32)[None, :] < length[:, None]
    steps_live = jnp.arange(step_count, dtype=jnp.int32)[None, :] <= jnp.arange(step_count, dtype=jnp.int32)[:, None]
    valid_mask = jnp.concatenate([
        jnp.broadcast_to(cache_live[:, None, :], (sample_count, step_count, slots)),
        jnp.broadcast_to(steps_live[None], (sample_count, step_count, step_count))], axis=2)
    return apply_weights(logit_scores, valid_mask[:, :, None, None, :], value_matrix, "stkgl,slkd->stkgd")


def join(former, latter):
    maxima = jnp.maximum(former[1], latter[1])
    scale_a = jnp.exp(former[1] - maxima)
    scale_b = jnp.exp(latter[1] - maxima)
    return (former[0] * scale_a[..., None] + latter[0] * scale_b[..., None], maxima, former[2] * scale_a + latter[2] * scale_b)


def reference(queries, new_kv, suffix_kv, suffix_len, prefix_head, prefix_tail, prefix_len):
    def one_prompt(prompt_index):
        query_rows = queries[prompt_index]
        whole = jnp.concatenate([prefix_head[prompt_index], prefix_tail[(prompt_index + 1) % PROMPTS]], axis=0)
        far_part = prefix_terms(query_rows, whole, jnp.int32(0), prefix_len[prompt_index])
        near_part = suffix_terms(query_rows, suffix_kv[prompt_index], new_kv[prompt_index], suffix_len[prompt_index])
        result = join(far_part, near_part)
        attended = (result[0] / result[2][..., None]).astype(jnp.bfloat16)
        return attended.reshape(query_rows.shape)

    return lax.map(one_prompt, jnp.arange(PROMPTS, dtype=jnp.int32))
```

```python
import jax
import jax.numpy as jnp
from jax import lax
from jax.sharding import PartitionSpec as P

QH = 64
KVH = 8
HEAD_SIZE = 128
GROUP = QH // KVH


NEG = -1e30


def shifted(value, axis, steps):
    count = lax.axis_size(axis)
    pairs = [(source, (source + steps) % count) for source in range(count)]
    return lax.ppermute(value, axis, pairs)


def split_dot(weights, value_matrix, form):
    rounded = lax.reduce_precision(weights, exponent_bits=8, mantissa_bits=7)
    high = rounded.astype(jnp.bfloat16)
    low = (weights - rounded).astype(jnp.bfloat16)
    return jnp.einsum(form, high, value_matrix, preferred_element_type=jnp.float32) + jnp.einsum(
        form, low, value_matrix, preferred_element_type=jnp.float32
    )


def softmax_terms(logit_scores, valid_mask, value_matrix, form):
    masked = jnp.where(valid_mask, logit_scores, NEG)
    maxima = jnp.max(masked, axis=-1)
    weights = jnp.where(valid_mask, jnp.exp(masked - maxima[..., None]), 0.0)
    totals = jnp.sum(weights, axis=-1)
    return split_dot(weights, value_matrix, form), maxima, totals


def suffix_terms(query_rows, cache, fresh, length):
    step_count = query_rows.shape[0]
    slots = cache.shape[0]
    grouped = query_rows.reshape(step_count, KVH, GROUP, HEAD_SIZE)
    cache_keys = cache[:, 0].reshape(slots, KVH, HEAD_SIZE)
    cache_values = cache[:, 1].reshape(slots, KVH, HEAD_SIZE)
    fresh_keys = fresh[:, 0].reshape(step_count, KVH, HEAD_SIZE)
    fresh_values = fresh[:, 1].reshape(step_count, KVH, HEAD_SIZE)
    scale = HEAD_SIZE ** (-0.5)
    cache_scores = jnp.einsum("tkgd,lkd->tkgl", grouped, cache_keys, preferred_element_type=jnp.float32) * scale
    fresh_scores = jnp.einsum("tkgd,ukd->tkgu", grouped, fresh_keys, preferred_element_type=jnp.float32) * scale
    cache_live = (jnp.arange(slots, dtype=jnp.int32) < length)[None, None, None, :]
    steps_live = (
        jnp.arange(step_count, dtype=jnp.int32)[None, :] <= jnp.arange(step_count, dtype=jnp.int32)[:, None]
    )[:, None, None, :]
    cache_masked = jnp.where(cache_live, cache_scores, NEG)
    fresh_masked = jnp.where(steps_live, fresh_scores, NEG)
    maxima = jnp.maximum(jnp.max(cache_masked, axis=-1), jnp.max(fresh_masked, axis=-1))
    cache_weights = jnp.where(cache_live, jnp.exp(cache_masked - maxima[..., None]), 0.0)
    fresh_weights = jnp.where(steps_live, jnp.exp(fresh_masked - maxima[..., None]), 0.0)
    totals = jnp.sum(cache_weights, axis=-1) + jnp.sum(fresh_weights, axis=-1)
    numerator = split_dot(cache_weights, cache_values, "tkgl,lkd->tkgd") + split_dot(
        fresh_weights, fresh_values, "tkgu,ukd->tkgd"
    )
    return (
        numerator.reshape(step_count, QH, HEAD_SIZE),
        maxima.reshape(step_count, QH),
        totals.reshape(step_count, QH),
    )


def per_device(queries, new_kv, suffix_kv, suffix_len, prefix_head, prefix_tail, prefix_len):
    sample_count = lax.axis_size("sample")
    prompt_count = lax.axis_size("prompt")
    prompt_row = lax.axis_index("prompt")
    sample_slot = lax.axis_index("sample")
    side = sample_slot % 2
    block_len = prefix_head.shape[1]
    half_len = block_len * sample_count
    step_count = queries.shape[2]

    def by_head(block):
        return block[0].reshape(block_len, 2, KVH, HEAD_SIZE).transpose(2, 1, 0, 3)

    outgoing_kv = jnp.stack([by_head(prefix_head), by_head(prefix_tail)], axis=1)
    outgoing_kv = outgoing_kv.reshape(2 * KVH, 2, block_len, HEAD_SIZE)
    gathered_kv = lax.all_to_all(outgoing_kv, "sample", 0, 0, tiled=True)
    keys = gathered_kv[:, 0].reshape(half_len, HEAD_SIZE)
    values = gathered_kv[:, 1].reshape(half_len, HEAD_SIZE)

    own_rows = queries[0, 0]
    previous_rows = shifted(own_rows, "prompt", 1)

    def query_groups(rows):
        return rows.reshape(step_count, KVH, GROUP, HEAD_SIZE).transpose(1, 0, 2, 3)

    outgoing_q = jnp.stack([query_groups(own_rows), query_groups(previous_rows)], axis=1)
    outgoing_q = outgoing_q.reshape(2 * KVH, step_count, GROUP, HEAD_SIZE)
    gathered_q = lax.all_to_all(outgoing_q, "sample", 0, 0, tiled=True)
    query_matrix = gathered_q.reshape(sample_count * step_count * GROUP, HEAD_SIZE)

    target_prompt = (prompt_row - side + prompt_count) % prompt_count
    length = prefix_len[target_prompt]
    positions = side * half_len + jnp.arange(half_len, dtype=jnp.int32)
    valid = (positions < length)[None, :]
    scores = jnp.einsum("rd,kd->rk", query_matrix, keys, preferred_element_type=jnp.float32) * HEAD_SIZE ** (-0.5)
    numerator, maxima, totals = softmax_terms(scores, valid, values, "rk,kd->rd")
    rows_per_sample = step_count * GROUP
    numerator = numerator.reshape(sample_count, rows_per_sample, HEAD_SIZE)
    stats = jnp.concatenate(
        [
            maxima.reshape(sample_count, rows_per_sample),
            totals.reshape(sample_count, rows_per_sample),
            jnp.zeros((sample_count, HEAD_SIZE - 2 * rows_per_sample), jnp.float32),
        ],
        axis=1,
    )
    outgoing_parts = jnp.concatenate([numerator, stats[:, None, :]], axis=1)
    returned = lax.all_to_all(outgoing_parts, "sample", 0, 0, tiled=True)
    returned = returned.reshape(KVH, 2, rows_per_sample + 1, HEAD_SIZE)
    head_parts = returned[:, 0]
    tail_parts = shifted(returned[:, 1], "prompt", -1)

    def unpack(parts):
        numer = parts[:, :rows_per_sample].reshape(KVH, step_count, GROUP, HEAD_SIZE)
        numer = numer.transpose(1, 0, 2, 3).reshape(step_count, QH, HEAD_SIZE)
        maxi = parts[:, rows_per_sample, :rows_per_sample].reshape(KVH, step_count, GROUP)
        maxi = maxi.transpose(1, 0, 2).reshape(step_count, QH)
        tot = parts[:, rows_per_sample, rows_per_sample : 2 * rows_per_sample].reshape(KVH, step_count, GROUP)
        tot = tot.transpose(1, 0, 2).reshape(step_count, QH)
        return numer, maxi, tot

    head_numer, head_max, head_tot = unpack(head_parts)
    tail_numer, tail_max, tail_tot = unpack(tail_parts)
    near_numer, near_max, near_tot = suffix_terms(own_rows, suffix_kv[0, 0], new_kv[0, 0], suffix_len[0, 0])

    top = jnp.maximum(jnp.maximum(head_max, tail_max), near_max)
    head_scale = jnp.exp(head_max - top)
    tail_scale = jnp.exp(tail_max - top)
    near_scale = jnp.exp(near_max - top)
    numer = (
        head_numer * head_scale[..., None] + tail_numer * tail_scale[..., None] + near_numer * near_scale[..., None]
    )
    total = head_tot * head_scale + tail_tot * tail_scale + near_tot * near_scale
    attended = (numer / total[..., None]).astype(jnp.bfloat16)
    return attended.reshape(queries.shape)


def solution(mesh):
    in_specs = (
        P("prompt", "sample", None, None),
        P("prompt", "sample", None, None, None),
        P("prompt", "sample", None, None, None),
        P("prompt", "sample"),
        P("prompt", "sample", None, None),
        P("prompt", "sample", None, None),
        P(),
    )
    out_specs = P("prompt", "sample", None, None)
    return jax.shard_map(
        per_device, mesh=mesh, in_specs=in_specs, out_specs=out_specs, check_vma=False
    )
```

```python
import jax
import jax.numpy as jnp
from jax import lax
from jax.sharding import PartitionSpec as P

QH = 64
KVH = 8
HEAD_SIZE = 128
GROUP = QH // KVH


NEG = -1e30


def shifted(value, axis, steps):
    count = lax.axis_size(axis)
    pairs = [(source, (source + steps) % count) for source in range(count)]
    return lax.ppermute(value, axis, pairs)


def split_dot(weights, value_matrix, form):
    rounded = lax.reduce_precision(weights, exponent_bits=8, mantissa_bits=7)
    high = rounded.astype(jnp.bfloat16)
    low = (weights - rounded).astype(jnp.bfloat16)
    return jnp.einsum(form, high, value_matrix, preferred_element_type=jnp.float32) + jnp.einsum(
        form, low, value_matrix, preferred_element_type=jnp.float32
    )


def softmax_terms(logit_scores, valid_mask, value_matrix, form):
    masked = jnp.where(valid_mask, logit_scores, NEG)
    maxima = jnp.max(masked, axis=-1)
    weights = jnp.where(valid_mask, jnp.exp(masked - maxima[..., None]), 0.0)
    totals = jnp.sum(weights, axis=-1)
    return split_dot(weights, value_matrix, form), maxima, totals


def suffix_terms(query_rows, cache, fresh, length):
    step_count = query_rows.shape[0]
    slots = cache.shape[0]
    grouped = query_rows.reshape(step_count, KVH, GROUP, HEAD_SIZE)
    cache_keys = cache[:, 0].reshape(slots, KVH, HEAD_SIZE)
    cache_values = cache[:, 1].reshape(slots, KVH, HEAD_SIZE)
    fresh_keys = fresh[:, 0].reshape(step_count, KVH, HEAD_SIZE)
    fresh_values = fresh[:, 1].reshape(step_count, KVH, HEAD_SIZE)
    scale = HEAD_SIZE ** (-0.5)
    cache_scores = jnp.einsum("tkgd,lkd->tkgl", grouped, cache_keys, preferred_element_type=jnp.float32) * scale
    fresh_scores = jnp.einsum("tkgd,ukd->tkgu", grouped, fresh_keys, preferred_element_type=jnp.float32) * scale
    cache_live = (jnp.arange(slots, dtype=jnp.int32) < length)[None, None, None, :]
    steps_live = (
        jnp.arange(step_count, dtype=jnp.int32)[None, :] <= jnp.arange(step_count, dtype=jnp.int32)[:, None]
    )[:, None, None, :]
    cache_masked = jnp.where(cache_live, cache_scores, NEG)
    fresh_masked = jnp.where(steps_live, fresh_scores, NEG)
    maxima = jnp.maximum(jnp.max(cache_masked, axis=-1), jnp.max(fresh_masked, axis=-1))
    cache_weights = jnp.where(cache_live, jnp.exp(cache_masked - maxima[..., None]), 0.0)
    fresh_weights = jnp.where(steps_live, jnp.exp(fresh_masked - maxima[..., None]), 0.0)
    totals = jnp.sum(cache_weights, axis=-1) + jnp.sum(fresh_weights, axis=-1)
    numerator = split_dot(cache_weights, cache_values, "tkgl,lkd->tkgd") + split_dot(
        fresh_weights, fresh_values, "tkgu,ukd->tkgd"
    )
    return (
        numerator.reshape(step_count, QH, HEAD_SIZE),
        maxima.reshape(step_count, QH),
        totals.reshape(step_count, QH),
    )


def per_device(queries, new_kv, suffix_kv, suffix_len, prefix_head, prefix_tail, prefix_len):
    sample_count = lax.axis_size("sample")
    prompt_row = lax.axis_index("prompt")
    sample_slot = lax.axis_index("sample")
    side = sample_slot % 2
    block_len = prefix_head.shape[1]
    half_len = block_len * sample_count
    step_count = queries.shape[2]

    moved_tail = shifted(prefix_tail, "prompt", -1)
    own_rows = queries[0, 0]

    def by_head(block):
        return block[0].reshape(block_len, 2, KVH, HEAD_SIZE).transpose(2, 1, 0, 3).reshape(KVH, 2 * block_len, HEAD_SIZE)

    query_groups = own_rows.reshape(step_count, KVH, GROUP, HEAD_SIZE).transpose(1, 0, 2, 3)
    query_groups = query_groups.reshape(KVH, step_count * GROUP, HEAD_SIZE)
    outgoing = jnp.stack(
        [
            jnp.concatenate([by_head(prefix_head), query_groups], axis=1),
            jnp.concatenate([by_head(moved_tail), query_groups], axis=1),
        ],
        axis=1,
    ).reshape(2 * KVH, 2 * block_len + step_count * GROUP, HEAD_SIZE)
    gathered = lax.all_to_all(outgoing, "sample", 0, 0, tiled=True)
    keys = gathered[:, :block_len].reshape(half_len, HEAD_SIZE)
    values = gathered[:, block_len : 2 * block_len].reshape(half_len, HEAD_SIZE)
    query_matrix = gathered[:, 2 * block_len :].reshape(sample_count * step_count * GROUP, HEAD_SIZE)

    length = prefix_len[prompt_row]
    positions = side * half_len + jnp.arange(half_len, dtype=jnp.int32)
    valid = (positions < length)[None, :]
    scores = jnp.einsum("rd,kd->rk", query_matrix, keys, preferred_element_type=jnp.float32) * HEAD_SIZE ** (-0.5)
    numerator, maxima, totals = softmax_terms(scores, valid, values, "rk,kd->rd")
    rows_per_sample = step_count * GROUP
    numerator = numerator.reshape(sample_count, rows_per_sample, HEAD_SIZE)
    stats = jnp.concatenate(
        [
            maxima.reshape(sample_count, rows_per_sample),
            totals.reshape(sample_count, rows_per_sample),
            jnp.zeros((sample_count, HEAD_SIZE - 2 * rows_per_sample), jnp.float32),
        ],
        axis=1,
    )
    outgoing_parts = jnp.concatenate([numerator, stats[:, None, :]], axis=1)
    returned = lax.all_to_all(outgoing_parts, "sample", 0, 0, tiled=True)
    returned = returned.reshape(KVH, 2, rows_per_sample + 1, HEAD_SIZE)
    head_parts = returned[:, 0]
    tail_parts = returned[:, 1]

    def unpack(parts):
        numer = parts[:, :rows_per_sample].reshape(KVH, step_count, GROUP, HEAD_SIZE)
        numer = numer.transpose(1, 0, 2, 3).reshape(step_count, QH, HEAD_SIZE)
        maxi = parts[:, rows_per_sample, :rows_per_sample].reshape(KVH, step_count, GROUP)
        maxi = maxi.transpose(1, 0, 2).reshape(step_count, QH)
        tot = parts[:, rows_per_sample, rows_per_sample : 2 * rows_per_sample].reshape(KVH, step_count, GROUP)
        tot = tot.transpose(1, 0, 2).reshape(step_count, QH)
        return numer, maxi, tot

    head_numer, head_max, head_tot = unpack(head_parts)
    tail_numer, tail_max, tail_tot = unpack(tail_parts)
    near_numer, near_max, near_tot = suffix_terms(own_rows, suffix_kv[0, 0], new_kv[0, 0], suffix_len[0, 0])

    top = jnp.maximum(jnp.maximum(head_max, tail_max), near_max)
    head_scale = jnp.exp(head_max - top)
    tail_scale = jnp.exp(tail_max - top)
    near_scale = jnp.exp(near_max - top)
    numer = (
        head_numer * head_scale[..., None] + tail_numer * tail_scale[..., None] + near_numer * near_scale[..., None]
    )
    total = head_tot * head_scale + tail_tot * tail_scale + near_tot * near_scale
    attended = (numer / total[..., None]).astype(jnp.bfloat16)
    return attended.reshape(queries.shape)


def solution(mesh):
    in_specs = (
        P("prompt", "sample", None, None),
        P("prompt", "sample", None, None, None),
        P("prompt", "sample", None, None, None),
        P("prompt", "sample"),
        P("prompt", "sample", None, None),
        P("prompt", "sample", None, None),
        P(),
    )
    out_specs = P("prompt", "sample", None, None)
    return jax.shard_map(
        per_device, mesh=mesh, in_specs=in_specs, out_specs=out_specs, check_vma=False
    )
```

```python
import jax
import jax.numpy as jnp
from jax import lax
from jax.sharding import PartitionSpec as P

QH = 64
KVH = 8
HEAD_SIZE = 128
GROUP = QH // KVH


NEG = -1e30


def shifted(value, axis, steps):
    count = lax.axis_size(axis)
    pairs = [(source, (source + steps) % count) for source in range(count)]
    return lax.ppermute(value, axis, pairs)


def split_dot(weights, value_matrix, form):
    rounded = lax.reduce_precision(weights, exponent_bits=8, mantissa_bits=7)
    high = rounded.astype(jnp.bfloat16)
    low = (weights - rounded).astype(jnp.bfloat16)
    return jnp.einsum(form, high, value_matrix, preferred_element_type=jnp.float32) + jnp.einsum(
        form, low, value_matrix, preferred_element_type=jnp.float32
    )


def softmax_terms(logit_scores, valid_mask, value_matrix, form):
    masked = jnp.where(valid_mask, logit_scores, NEG)
    maxima = jnp.max(masked, axis=-1)
    weights = jnp.where(valid_mask, jnp.exp(masked - maxima[..., None]), 0.0)
    totals = jnp.sum(weights, axis=-1)
    return split_dot(weights, value_matrix, form), maxima, totals


def suffix_terms(query_rows, cache, fresh, length):
    step_count = query_rows.shape[0]
    slots = cache.shape[0]
    grouped = query_rows.reshape(step_count, KVH, GROUP, HEAD_SIZE)
    cache_keys = cache[:, 0].reshape(slots, KVH, HEAD_SIZE)
    cache_values = cache[:, 1].reshape(slots, KVH, HEAD_SIZE)
    fresh_keys = fresh[:, 0].reshape(step_count, KVH, HEAD_SIZE)
    fresh_values = fresh[:, 1].reshape(step_count, KVH, HEAD_SIZE)
    scale = HEAD_SIZE ** (-0.5)
    cache_scores = jnp.einsum("tkgd,lkd->tkgl", grouped, cache_keys, preferred_element_type=jnp.float32) * scale
    fresh_scores = jnp.einsum("tkgd,ukd->tkgu", grouped, fresh_keys, preferred_element_type=jnp.float32) * scale
    cache_live = (jnp.arange(slots, dtype=jnp.int32) < length)[None, None, None, :]
    steps_live = (
        jnp.arange(step_count, dtype=jnp.int32)[None, :] <= jnp.arange(step_count, dtype=jnp.int32)[:, None]
    )[:, None, None, :]
    cache_masked = jnp.where(cache_live, cache_scores, NEG)
    fresh_masked = jnp.where(steps_live, fresh_scores, NEG)
    maxima = jnp.maximum(jnp.max(cache_masked, axis=-1), jnp.max(fresh_masked, axis=-1))
    cache_weights = jnp.where(cache_live, jnp.exp(cache_masked - maxima[..., None]), 0.0)
    fresh_weights = jnp.where(steps_live, jnp.exp(fresh_masked - maxima[..., None]), 0.0)
    totals = jnp.sum(cache_weights, axis=-1) + jnp.sum(fresh_weights, axis=-1)
    numerator = split_dot(cache_weights, cache_values, "tkgl,lkd->tkgd") + split_dot(
        fresh_weights, fresh_values, "tkgu,ukd->tkgd"
    )
    return (
        numerator.reshape(step_count, QH, HEAD_SIZE),
        maxima.reshape(step_count, QH),
        totals.reshape(step_count, QH),
    )


def per_device(queries, new_kv, suffix_kv, suffix_len, prefix_head, prefix_tail, prefix_len):
    team_count = lax.axis_size(("zl", "core"))
    prompt_row = lax.axis_index("prompt")
    team = lax.axis_index("zg")
    block_len = prefix_head.shape[1]
    step_count = queries.shape[2]
    rows_per_sample = step_count * GROUP

    moved_tail = shifted(prefix_tail, "prompt", -1)
    own_rows = queries[0, 0]
    partner_rows = shifted(own_rows, "zg", 1)

    halves = jnp.stack(
        [prefix_head[0].reshape(block_len, 2, KVH, HEAD_SIZE), moved_tail[0].reshape(block_len, 2, KVH, HEAD_SIZE)]
    )
    kv_part = halves.transpose(3, 2, 0, 1, 4).reshape(KVH, 2 * 2 * block_len, HEAD_SIZE)

    def query_groups(rows):
        return rows.reshape(step_count, KVH, GROUP, HEAD_SIZE).transpose(1, 0, 2, 3).reshape(KVH, rows_per_sample, HEAD_SIZE)

    outgoing = jnp.concatenate([kv_part, query_groups(own_rows), query_groups(partner_rows)], axis=1)
    gathered = lax.all_to_all(outgoing, ("zl", "core"), 0, 0, tiled=True)
    span = 2 * block_len
    keys = gathered[:, :span].reshape(team_count * span, HEAD_SIZE)
    values = gathered[:, span : 2 * span].reshape(team_count * span, HEAD_SIZE)
    query_parts = gathered[:, 2 * span :].reshape(team_count, 2, rows_per_sample, HEAD_SIZE).transpose(1, 0, 2, 3)
    query_parts = jnp.where(team == 0, query_parts, query_parts[::-1])
    query_matrix = query_parts.reshape(2 * team_count * rows_per_sample, HEAD_SIZE)

    member = jnp.arange(team_count, dtype=jnp.int32)[:, None, None]
    half = jnp.arange(2, dtype=jnp.int32)[None, :, None]
    offset = jnp.arange(block_len, dtype=jnp.int32)[None, None, :]
    prefix_half_len = block_len * team_count * 2
    positions = half * prefix_half_len + (team * team_count + member) * block_len + offset
    valid = (positions.reshape(-1) < prefix_len[prompt_row])[None, :]
    scores = jnp.einsum("rd,kd->rk", query_matrix, keys, preferred_element_type=jnp.float32) * HEAD_SIZE ** (-0.5)
    numerator, maxima, totals = softmax_terms(scores, valid, values, "rk,kd->rd")
    sample_count = 2 * team_count
    numerator = numerator.reshape(sample_count, rows_per_sample, HEAD_SIZE)
    stats = jnp.concatenate(
        [
            maxima.reshape(sample_count, rows_per_sample),
            totals.reshape(sample_count, rows_per_sample),
            jnp.zeros((sample_count, HEAD_SIZE - 2 * rows_per_sample), jnp.float32),
        ],
        axis=1,
    )
    outgoing_parts = jnp.concatenate([numerator, stats[:, None, :]], axis=1)
    returned = lax.all_to_all(outgoing_parts, ("zg", "zl", "core"), 0, 0, tiled=True)
    returned = returned.reshape(2, KVH, rows_per_sample + 1, HEAD_SIZE)

    def unpack(parts):
        numer = parts[:, :rows_per_sample].reshape(KVH, step_count, GROUP, HEAD_SIZE)
        numer = numer.transpose(1, 0, 2, 3).reshape(step_count, QH, HEAD_SIZE)
        maxi = parts[:, rows_per_sample, :rows_per_sample].reshape(KVH, step_count, GROUP)
        maxi = maxi.transpose(1, 0, 2).reshape(step_count, QH)
        tot = parts[:, rows_per_sample, rows_per_sample : 2 * rows_per_sample].reshape(KVH, step_count, GROUP)
        tot = tot.transpose(1, 0, 2).reshape(step_count, QH)
        return numer, maxi, tot

    first_numer, first_max, first_tot = unpack(returned[0])
    second_numer, second_max, second_tot = unpack(returned[1])
    near_numer, near_max, near_tot = suffix_terms(own_rows, suffix_kv[0, 0], new_kv[0, 0], suffix_len[0, 0])

    top = jnp.maximum(jnp.maximum(first_max, second_max), near_max)
    first_scale = jnp.exp(first_max - top)
    second_scale = jnp.exp(second_max - top)
    near_scale = jnp.exp(near_max - top)
    numer = (
        first_numer * first_scale[..., None]
        + second_numer * second_scale[..., None]
        + near_numer * near_scale[..., None]
    )
    total = first_tot * first_scale + second_tot * second_scale + near_tot * near_scale
    attended = (numer / total[..., None]).astype(jnp.bfloat16)
    return attended.reshape(queries.shape)


def solution(mesh):
    prompts, samples = mesh.devices.shape
    teams = 2
    team_mesh = jax.sharding.Mesh(
        mesh.devices.reshape(prompts, teams, samples // (2 * teams), 2), ("prompt", "zg", "zl", "core")
    )
    spread = ("zg", "zl", "core")
    in_specs = (
        P("prompt", spread, None, None),
        P("prompt", spread, None, None, None),
        P("prompt", spread, None, None, None),
        P("prompt", spread),
        P("prompt", spread, None, None),
        P("prompt", spread, None, None),
        P(),
    )
    out_specs = P("prompt", spread, None, None)
    return jax.shard_map(
        per_device, mesh=team_mesh, in_specs=in_specs, out_specs=out_specs, check_vma=False
    )
```

```python
import jax
import jax.numpy as jnp
from jax import lax
from jax.experimental import pallas as pl
from jax.sharding import PartitionSpec as P

QH = 64
KVH = 8
HEAD_SIZE = 128
GROUP = QH // KVH


NEG = -1e30
ROW_BLOCK = 128


def prefix_kernel(live_ref, query_ref, key_ref, value_ref, numer_ref, max_ref, total_ref):
    scores = lax.dot_general(
        query_ref[...], key_ref[...], (((1,), (1,)), ((), ())), preferred_element_type=jnp.float32
    ) * HEAD_SIZE ** (-0.5)
    live = live_ref[...] > 0
    masked = jnp.where(live, scores, NEG)
    maxima = jnp.max(masked, axis=1, keepdims=True)
    weights = jnp.where(live, jnp.exp(masked - maxima), 0.0)
    max_ref[...] = maxima
    total_ref[...] = jnp.sum(weights, axis=1, keepdims=True)
    high = weights.astype(jnp.bfloat16)
    low = (weights - high.astype(jnp.float32)).astype(jnp.bfloat16)
    values = value_ref[...]
    numer_ref[...] = jnp.dot(high, values, preferred_element_type=jnp.float32) + jnp.dot(
        low, values, preferred_element_type=jnp.float32
    )


def prefix_attention(live, query_matrix, keys, values):
    rows, width = query_matrix.shape
    span = keys.shape[0]
    return pl.pallas_call(
        prefix_kernel,
        grid=(rows // ROW_BLOCK,),
        in_specs=[
            pl.BlockSpec((1, span), lambda i: (0, 0)),
            pl.BlockSpec((ROW_BLOCK, width), lambda i: (i, 0)),
            pl.BlockSpec((span, width), lambda i: (0, 0)),
            pl.BlockSpec((span, width), lambda i: (0, 0)),
        ],
        out_specs=[
            pl.BlockSpec((ROW_BLOCK, width), lambda i: (i, 0)),
            pl.BlockSpec((ROW_BLOCK, 1), lambda i: (i, 0)),
            pl.BlockSpec((ROW_BLOCK, 1), lambda i: (i, 0)),
        ],
        out_shape=[
            jax.ShapeDtypeStruct((rows, width), jnp.float32),
            jax.ShapeDtypeStruct((rows, 1), jnp.float32),
            jax.ShapeDtypeStruct((rows, 1), jnp.float32),
        ],
        cost_estimate=pl.CostEstimate(
            flops=6 * rows * span * width, transcendentals=rows * span, bytes_accessed=2 * (rows + 2 * span) * width + 8 * rows * width
        ),
    )(live, query_matrix, keys, values)


def shifted(value, axis, steps):
    count = lax.axis_size(axis)
    pairs = [(source, (source + steps) % count) for source in range(count)]
    return lax.ppermute(value, axis, pairs)


def split_dot(weights, value_matrix, form):
    rounded = lax.reduce_precision(weights, exponent_bits=8, mantissa_bits=7)
    high = rounded.astype(jnp.bfloat16)
    low = (weights - rounded).astype(jnp.bfloat16)
    return jnp.einsum(form, high, value_matrix, preferred_element_type=jnp.float32) + jnp.einsum(
        form, low, value_matrix, preferred_element_type=jnp.float32
    )


def suffix_terms(query_rows, cache, fresh, length):
    step_count = query_rows.shape[0]
    slots = cache.shape[0]
    grouped = query_rows.reshape(step_count, KVH, GROUP, HEAD_SIZE)
    cache_keys = cache[:, 0].reshape(slots, KVH, HEAD_SIZE)
    cache_values = cache[:, 1].reshape(slots, KVH, HEAD_SIZE)
    fresh_keys = fresh[:, 0].reshape(step_count, KVH, HEAD_SIZE)
    fresh_values = fresh[:, 1].reshape(step_count, KVH, HEAD_SIZE)
    scale = HEAD_SIZE ** (-0.5)
    cache_scores = jnp.einsum("tkgd,lkd->tkgl", grouped, cache_keys, preferred_element_type=jnp.float32) * scale
    fresh_scores = jnp.einsum("tkgd,ukd->tkgu", grouped, fresh_keys, preferred_element_type=jnp.float32) * scale
    cache_live = (jnp.arange(slots, dtype=jnp.int32) < length)[None, None, None, :]
    steps_live = (
        jnp.arange(step_count, dtype=jnp.int32)[None, :] <= jnp.arange(step_count, dtype=jnp.int32)[:, None]
    )[:, None, None, :]
    cache_masked = jnp.where(cache_live, cache_scores, NEG)
    fresh_masked = jnp.where(steps_live, fresh_scores, NEG)
    maxima = jnp.maximum(jnp.max(cache_masked, axis=-1), jnp.max(fresh_masked, axis=-1))
    cache_weights = jnp.where(cache_live, jnp.exp(cache_masked - maxima[..., None]), 0.0)
    fresh_weights = jnp.where(steps_live, jnp.exp(fresh_masked - maxima[..., None]), 0.0)
    totals = jnp.sum(cache_weights, axis=-1) + jnp.sum(fresh_weights, axis=-1)
    numerator = split_dot(cache_weights, cache_values, "tkgl,lkd->tkgd") + split_dot(
        fresh_weights, fresh_values, "tkgu,ukd->tkgd"
    )
    return (
        numerator.reshape(step_count, QH, HEAD_SIZE),
        maxima.reshape(step_count, QH),
        totals.reshape(step_count, QH),
    )


def per_device(queries, new_kv, suffix_kv, suffix_len, prefix_head, prefix_tail, prefix_len):
    team_count = lax.axis_size(("zl", "core"))
    prompt_row = lax.axis_index("prompt")
    team = lax.axis_index("zg")
    block_len = prefix_head.shape[1]
    step_count = queries.shape[2]
    rows_per_sample = step_count * GROUP

    moved_tail = shifted(prefix_tail, "prompt", -1)
    own_rows = queries[0, 0]
    partner_rows = shifted(own_rows, "zg", 1)

    halves = jnp.stack(
        [prefix_head[0].reshape(block_len, 2, KVH, HEAD_SIZE), moved_tail[0].reshape(block_len, 2, KVH, HEAD_SIZE)]
    )
    kv_part = halves.transpose(3, 2, 0, 1, 4).reshape(KVH, 2 * 2 * block_len, HEAD_SIZE)

    def query_groups(rows):
        return rows.reshape(step_count, KVH, GROUP, HEAD_SIZE).transpose(1, 0, 2, 3).reshape(KVH, rows_per_sample, HEAD_SIZE)

    outgoing = jnp.concatenate([kv_part, query_groups(own_rows), query_groups(partner_rows)], axis=1)
    gathered = lax.all_to_all(outgoing, ("zl", "core"), 0, 0, tiled=True)
    span = 2 * block_len
    keys = gathered[:, :span].reshape(team_count * span, HEAD_SIZE)
    values = gathered[:, span : 2 * span].reshape(team_count * span, HEAD_SIZE)
    query_parts = gathered[:, 2 * span :].reshape(team_count, 2, rows_per_sample, HEAD_SIZE).transpose(1, 0, 2, 3)
    query_parts = jnp.where(team == 0, query_parts, query_parts[::-1])
    query_matrix = query_parts.reshape(2 * team_count * rows_per_sample, HEAD_SIZE)

    member = jnp.arange(team_count, dtype=jnp.int32)[:, None, None]
    half = jnp.arange(2, dtype=jnp.int32)[None, :, None]
    offset = jnp.arange(block_len, dtype=jnp.int32)[None, None, :]
    prefix_half_len = block_len * team_count * 2
    positions = half * prefix_half_len + (team * team_count + member) * block_len + offset
    live = (positions.reshape(1, -1) < prefix_len[prompt_row]).astype(jnp.int32)
    numerator, maxima, totals = prefix_attention(live, query_matrix, keys, values)
    sample_count = 2 * team_count
    numerator = numerator.reshape(sample_count, rows_per_sample, HEAD_SIZE)
    stats = jnp.concatenate(
        [
            maxima.reshape(sample_count, rows_per_sample),
            totals.reshape(sample_count, rows_per_sample),
            jnp.zeros((sample_count, HEAD_SIZE - 2 * rows_per_sample), jnp.float32),
        ],
        axis=1,
    )
    outgoing_parts = jnp.concatenate([numerator, stats[:, None, :]], axis=1)
    returned = lax.all_to_all(outgoing_parts, ("zg", "zl", "core"), 0, 0, tiled=True)
    returned = returned.reshape(2, KVH, rows_per_sample + 1, HEAD_SIZE)

    def unpack(parts):
        numer = parts[:, :rows_per_sample].reshape(KVH, step_count, GROUP, HEAD_SIZE)
        numer = numer.transpose(1, 0, 2, 3).reshape(step_count, QH, HEAD_SIZE)
        maxi = parts[:, rows_per_sample, :rows_per_sample].reshape(KVH, step_count, GROUP)
        maxi = maxi.transpose(1, 0, 2).reshape(step_count, QH)
        tot = parts[:, rows_per_sample, rows_per_sample : 2 * rows_per_sample].reshape(KVH, step_count, GROUP)
        tot = tot.transpose(1, 0, 2).reshape(step_count, QH)
        return numer, maxi, tot

    first_numer, first_max, first_tot = unpack(returned[0])
    second_numer, second_max, second_tot = unpack(returned[1])
    near_numer, near_max, near_tot = suffix_terms(own_rows, suffix_kv[0, 0], new_kv[0, 0], suffix_len[0, 0])

    top = jnp.maximum(jnp.maximum(first_max, second_max), near_max)
    first_scale = jnp.exp(first_max - top)
    second_scale = jnp.exp(second_max - top)
    near_scale = jnp.exp(near_max - top)
    numer = (
        first_numer * first_scale[..., None]
        + second_numer * second_scale[..., None]
        + near_numer * near_scale[..., None]
    )
    total = first_tot * first_scale + second_tot * second_scale + near_tot * near_scale
    attended = (numer / total[..., None]).astype(jnp.bfloat16)
    return attended.reshape(queries.shape)


def solution(mesh):
    prompts, samples = mesh.devices.shape
    teams = 2
    team_mesh = jax.sharding.Mesh(
        mesh.devices.reshape(prompts, teams, samples // (2 * teams), 2), ("prompt", "zg", "zl", "core")
    )
    spread = ("zg", "zl", "core")
    in_specs = (
        P("prompt", spread, None, None),
        P("prompt", spread, None, None, None),
        P("prompt", spread, None, None, None),
        P("prompt", spread),
        P("prompt", spread, None, None),
        P("prompt", spread, None, None),
        P(),
    )
    out_specs = P("prompt", spread, None, None)
    return jax.shard_map(
        per_device, mesh=team_mesh, in_specs=in_specs, out_specs=out_specs, check_vma=False
    )
```

```python
import jax
import jax.numpy as jnp
from jax import lax
from jax.experimental import pallas as pl
from jax.sharding import PartitionSpec as P

QH = 64
KVH = 8
HEAD_SIZE = 128
GROUP = QH // KVH


NEG = -1e30
ROW_BLOCK = 128


def prefix_kernel(bias_ref, query_ref, key_ref, value_ref, out_ref):
    scores = lax.dot_general(
        query_ref[...], key_ref[...], (((1,), (1,)), ((), ())), preferred_element_type=jnp.float32
    ) * HEAD_SIZE ** (-0.5) + bias_ref[...]
    maxima = jnp.max(scores, axis=1, keepdims=True)
    weights = jnp.exp(scores - maxima)
    totals = jnp.sum(weights, axis=1, keepdims=True)
    high = weights.astype(jnp.bfloat16)
    low = (weights - high.astype(jnp.float32)).astype(jnp.bfloat16)
    values = value_ref[...]
    numer = jnp.dot(high, values, preferred_element_type=jnp.float32) + jnp.dot(
        low, values, preferred_element_type=jnp.float32
    )
    samples, rows, width = out_ref.shape
    rows = rows - 2
    out_ref[:, :rows, :] = numer.reshape(samples, rows, width)
    max_row = jnp.transpose(jnp.broadcast_to(maxima, (ROW_BLOCK, ROW_BLOCK)))[0:1, :]
    total_row = jnp.transpose(jnp.broadcast_to(totals, (ROW_BLOCK, ROW_BLOCK)))[0:1, :]
    out_ref[:, rows : rows + 1, :] = jnp.broadcast_to(max_row[None], (samples, 1, width))
    out_ref[:, rows + 1 : rows + 2, :] = jnp.broadcast_to(total_row[None], (samples, 1, width))


def prefix_attention(bias, query_matrix, keys, values, rows_per_sample):
    rows, width = query_matrix.shape
    span = keys.shape[0]
    per_block = ROW_BLOCK // rows_per_sample
    return pl.pallas_call(
        prefix_kernel,
        grid=(rows // ROW_BLOCK,),
        in_specs=[
            pl.BlockSpec((1, span), lambda i: (0, 0)),
            pl.BlockSpec((ROW_BLOCK, width), lambda i: (i, 0)),
            pl.BlockSpec((span, width), lambda i: (0, 0)),
            pl.BlockSpec((span, width), lambda i: (0, 0)),
        ],
        out_specs=pl.BlockSpec((per_block, rows_per_sample + 2, width), lambda i: (i, 0, 0)),
        out_shape=jax.ShapeDtypeStruct((rows // rows_per_sample, rows_per_sample + 2, width), jnp.float32),
        cost_estimate=pl.CostEstimate(
            flops=6 * rows * span * width, transcendentals=rows * span, bytes_accessed=2 * (rows + 2 * span) * width + 4 * rows * width
        ),
    )(bias, query_matrix, keys, values)


def shifted(value, axis, steps):
    count = lax.axis_size(axis)
    pairs = [(source, (source + steps) % count) for source in range(count)]
    return lax.ppermute(value, axis, pairs)


def split_dot(weights, value_matrix, form):
    rounded = lax.reduce_precision(weights, exponent_bits=8, mantissa_bits=7)
    high = rounded.astype(jnp.bfloat16)
    low = (weights - rounded).astype(jnp.bfloat16)
    return jnp.einsum(form, high, value_matrix, preferred_element_type=jnp.float32) + jnp.einsum(
        form, low, value_matrix, preferred_element_type=jnp.float32
    )


def suffix_terms(query_rows, cache, fresh, length):
    step_count = query_rows.shape[0]
    slots = cache.shape[0]
    grouped = query_rows.reshape(step_count, KVH, GROUP, HEAD_SIZE)
    cache_keys = cache[:, 0].reshape(slots, KVH, HEAD_SIZE)
    cache_values = cache[:, 1].reshape(slots, KVH, HEAD_SIZE)
    fresh_keys = fresh[:, 0].reshape(step_count, KVH, HEAD_SIZE)
    fresh_values = fresh[:, 1].reshape(step_count, KVH, HEAD_SIZE)
    scale = HEAD_SIZE ** (-0.5)
    cache_scores = jnp.einsum("tkgd,lkd->tkgl", grouped, cache_keys, preferred_element_type=jnp.float32) * scale
    fresh_scores = jnp.einsum("tkgd,ukd->tkgu", grouped, fresh_keys, preferred_element_type=jnp.float32) * scale
    cache_live = (jnp.arange(slots, dtype=jnp.int32) < length)[None, None, None, :]
    steps_live = (
        jnp.arange(step_count, dtype=jnp.int32)[None, :] <= jnp.arange(step_count, dtype=jnp.int32)[:, None]
    )[:, None, None, :]
    cache_masked = jnp.where(cache_live, cache_scores, NEG)
    fresh_masked = jnp.where(steps_live, fresh_scores, NEG)
    maxima = jnp.maximum(jnp.max(cache_masked, axis=-1), jnp.max(fresh_masked, axis=-1))
    cache_weights = jnp.where(cache_live, jnp.exp(cache_masked - maxima[..., None]), 0.0)
    fresh_weights = jnp.where(steps_live, jnp.exp(fresh_masked - maxima[..., None]), 0.0)
    totals = jnp.sum(cache_weights, axis=-1) + jnp.sum(fresh_weights, axis=-1)
    numerator = split_dot(cache_weights, cache_values, "tkgl,lkd->tkgd") + split_dot(
        fresh_weights, fresh_values, "tkgu,ukd->tkgd"
    )
    return (
        numerator.reshape(step_count, QH, HEAD_SIZE),
        maxima.reshape(step_count, QH),
        totals.reshape(step_count, QH),
    )


def per_device(queries, new_kv, suffix_kv, suffix_len, prefix_head, prefix_tail, prefix_len):
    team_count = lax.axis_size(("zl", "core"))
    prompt_row = lax.axis_index("prompt")
    team = lax.axis_index("zg")
    block_len = prefix_head.shape[1]
    step_count = queries.shape[2]
    rows_per_sample = step_count * GROUP

    moved_tail = shifted(prefix_tail, "prompt", -1)
    own_rows = queries[0, 0]
    partner_rows = shifted(own_rows, "zg", 1)

    halves = jnp.stack(
        [prefix_head[0].reshape(block_len, 2, KVH, HEAD_SIZE), moved_tail[0].reshape(block_len, 2, KVH, HEAD_SIZE)]
    )
    kv_part = halves.transpose(3, 2, 0, 1, 4).reshape(KVH, 2 * 2 * block_len, HEAD_SIZE)

    def query_groups(rows):
        return rows.reshape(step_count, KVH, GROUP, HEAD_SIZE).transpose(1, 0, 2, 3).reshape(KVH, rows_per_sample, HEAD_SIZE)

    outgoing = jnp.concatenate([kv_part, query_groups(own_rows), query_groups(partner_rows)], axis=1)
    gathered = lax.all_to_all(outgoing, ("zl", "core"), 0, 0, tiled=True)
    span = 2 * block_len
    keys = gathered[:, :span].reshape(team_count * span, HEAD_SIZE)
    values = gathered[:, span : 2 * span].reshape(team_count * span, HEAD_SIZE)
    query_parts = gathered[:, 2 * span :].reshape(team_count, 2, rows_per_sample, HEAD_SIZE).transpose(1, 0, 2, 3)
    query_parts = jnp.where(team == 0, query_parts, query_parts[::-1])
    query_matrix = query_parts.reshape(2 * team_count * rows_per_sample, HEAD_SIZE)

    member = jnp.arange(team_count, dtype=jnp.int32)[:, None, None]
    half = jnp.arange(2, dtype=jnp.int32)[None, :, None]
    offset = jnp.arange(block_len, dtype=jnp.int32)[None, None, :]
    prefix_half_len = block_len * team_count * 2
    positions = half * prefix_half_len + (team * team_count + member) * block_len + offset
    bias = jnp.where(positions.reshape(1, -1) < prefix_len[prompt_row], 0.0, NEG).astype(jnp.float32)
    sample_count = 2 * team_count
    outgoing_parts = prefix_attention(bias, query_matrix, keys, values, rows_per_sample)
    returned = lax.all_to_all(outgoing_parts, ("zg", "zl", "core"), 0, 0, tiled=True)
    returned = returned.reshape(2, KVH, rows_per_sample + 2, HEAD_SIZE)
    lane_offset = (lax.axis_index(("zg", "zl", "core")) % (ROW_BLOCK // rows_per_sample)) * rows_per_sample

    def unpack(parts):
        numer = parts[:, :rows_per_sample].reshape(KVH, step_count, GROUP, HEAD_SIZE)
        numer = numer.transpose(1, 0, 2, 3).reshape(step_count, QH, HEAD_SIZE)
        maxi = lax.dynamic_slice_in_dim(parts[:, rows_per_sample], lane_offset, rows_per_sample, axis=1)
        maxi = maxi.reshape(KVH, step_count, GROUP)
        maxi = maxi.transpose(1, 0, 2).reshape(step_count, QH)
        tot = lax.dynamic_slice_in_dim(parts[:, rows_per_sample + 1], lane_offset, rows_per_sample, axis=1)
        tot = tot.reshape(KVH, step_count, GROUP)
        tot = tot.transpose(1, 0, 2).reshape(step_count, QH)
        return numer, maxi, tot

    first_numer, first_max, first_tot = unpack(returned[0])
    second_numer, second_max, second_tot = unpack(returned[1])
    near_numer, near_max, near_tot = suffix_terms(own_rows, suffix_kv[0, 0], new_kv[0, 0], suffix_len[0, 0])

    top = jnp.maximum(jnp.maximum(first_max, second_max), near_max)
    first_scale = jnp.exp(first_max - top)
    second_scale = jnp.exp(second_max - top)
    near_scale = jnp.exp(near_max - top)
    numer = (
        first_numer * first_scale[..., None]
        + second_numer * second_scale[..., None]
        + near_numer * near_scale[..., None]
    )
    total = first_tot * first_scale + second_tot * second_scale + near_tot * near_scale
    attended = (numer / total[..., None]).astype(jnp.bfloat16)
    return attended.reshape(queries.shape)


def solution(mesh):
    prompts, samples = mesh.devices.shape
    teams = 2
    team_mesh = jax.sharding.Mesh(
        mesh.devices.reshape(prompts, teams, samples // (2 * teams), 2), ("prompt", "zg", "zl", "core")
    )
    spread = ("zg", "zl", "core")
    in_specs = (
        P("prompt", spread, None, None),
        P("prompt", spread, None, None, None),
        P("prompt", spread, None, None, None),
        P("prompt", spread),
        P("prompt", spread, None, None),
        P("prompt", spread, None, None),
        P(),
    )
    out_specs = P("prompt", spread, None, None)
    return jax.shard_map(
        per_device, mesh=team_mesh, in_specs=in_specs, out_specs=out_specs, check_vma=False
    )
```

```python
import functools

import jax
import jax.numpy as jnp
from jax import lax
from jax.experimental import pallas as pl
from jax.sharding import PartitionSpec as P

QH = 64
KVH = 8
HEAD_SIZE = 128
GROUP = QH // KVH


NEG = -1e30
ROW_BLOCK = 128


def prefix_kernel(block, bias_ref, query_ref, first_ref, second_ref, out_ref):
    query = query_ref[...]
    members = first_ref.shape[0]
    parts = []
    for index, source in enumerate((first_ref, second_ref)):
        keys = source[:, :block, :].reshape(members * block, HEAD_SIZE)
        values = source[:, block : 2 * block, :].reshape(members * block, HEAD_SIZE)
        scores = lax.dot_general(
            query, keys, (((1,), (1,)), ((), ())), preferred_element_type=jnp.float32
        ) * HEAD_SIZE ** (-0.5) + bias_ref[index : index + 1, :]
        parts.append((scores, values))
    maxima = jnp.maximum(
        jnp.max(parts[0][0], axis=1, keepdims=True), jnp.max(parts[1][0], axis=1, keepdims=True)
    )
    numer = None
    totals = None
    for scores, values in parts:
        weights = jnp.exp(scores - maxima)
        part_total = jnp.sum(weights, axis=1, keepdims=True)
        high = weights.astype(jnp.bfloat16)
        low = (weights - high.astype(jnp.float32)).astype(jnp.bfloat16)
        part = jnp.dot(high, values, preferred_element_type=jnp.float32) + jnp.dot(
            low, values, preferred_element_type=jnp.float32
        )
        numer = part if numer is None else numer + part
        totals = part_total if totals is None else totals + part_total
    samples, rows, width = out_ref.shape
    rows = rows - 2
    out_ref[:, :rows, :] = numer.reshape(samples, rows, width)
    max_row = jnp.transpose(jnp.broadcast_to(maxima, (ROW_BLOCK, ROW_BLOCK)))[0:1, :]
    total_row = jnp.transpose(jnp.broadcast_to(totals, (ROW_BLOCK, ROW_BLOCK)))[0:1, :]
    out_ref[:, rows : rows + 1, :] = jnp.broadcast_to(max_row[None], (samples, 1, width))
    out_ref[:, rows + 1 : rows + 2, :] = jnp.broadcast_to(total_row[None], (samples, 1, width))


def prefix_attention(bias, query_matrix, first, second, block, rows_per_sample):
    rows, width = query_matrix.shape
    span = first.shape[0] * block
    per_block = ROW_BLOCK // rows_per_sample
    return pl.pallas_call(
        functools.partial(prefix_kernel, block),
        grid=(rows // ROW_BLOCK,),
        in_specs=[
            pl.BlockSpec(bias.shape, lambda i: (0, 0)),
            pl.BlockSpec((ROW_BLOCK, width), lambda i: (i, 0)),
            pl.BlockSpec(first.shape, lambda i: (0, 0, 0)),
            pl.BlockSpec(second.shape, lambda i: (0, 0, 0)),
        ],
        out_specs=pl.BlockSpec((per_block, rows_per_sample + 2, width), lambda i: (i, 0, 0)),
        out_shape=jax.ShapeDtypeStruct((rows // rows_per_sample, rows_per_sample + 2, width), jnp.float32),
        cost_estimate=pl.CostEstimate(
            flops=3 * rows * span * width, transcendentals=rows * span // 2, bytes_accessed=2 * (rows + span) * width + 4 * rows * width
        ),
    )(bias, query_matrix, first, second)


def shifted(value, axis, steps):
    count = lax.axis_size(axis)
    pairs = [(source, (source + steps) % count) for source in range(count)]
    return lax.ppermute(value, axis, pairs)


def split_dot(weights, value_matrix, form):
    rounded = lax.reduce_precision(weights, exponent_bits=8, mantissa_bits=7)
    high = rounded.astype(jnp.bfloat16)
    low = (weights - rounded).astype(jnp.bfloat16)
    return jnp.einsum(form, high, value_matrix, preferred_element_type=jnp.float32) + jnp.einsum(
        form, low, value_matrix, preferred_element_type=jnp.float32
    )


def suffix_terms(query_rows, cache, fresh, length):
    step_count = query_rows.shape[0]
    slots = cache.shape[0]
    grouped = query_rows.reshape(step_count, KVH, GROUP, HEAD_SIZE)
    cache_keys = cache[:, 0].reshape(slots, KVH, HEAD_SIZE)
    cache_values = cache[:, 1].reshape(slots, KVH, HEAD_SIZE)
    fresh_keys = fresh[:, 0].reshape(step_count, KVH, HEAD_SIZE)
    fresh_values = fresh[:, 1].reshape(step_count, KVH, HEAD_SIZE)
    scale = HEAD_SIZE ** (-0.5)
    cache_scores = jnp.einsum("tkgd,lkd->tkgl", grouped, cache_keys, preferred_element_type=jnp.float32) * scale
    fresh_scores = jnp.einsum("tkgd,ukd->tkgu", grouped, fresh_keys, preferred_element_type=jnp.float32) * scale
    cache_live = (jnp.arange(slots, dtype=jnp.int32) < length)[None, None, None, :]
    steps_live = (
        jnp.arange(step_count, dtype=jnp.int32)[None, :] <= jnp.arange(step_count, dtype=jnp.int32)[:, None]
    )[:, None, None, :]
    cache_masked = jnp.where(cache_live, cache_scores, NEG)
    fresh_masked = jnp.where(steps_live, fresh_scores, NEG)
    maxima = jnp.maximum(jnp.max(cache_masked, axis=-1), jnp.max(fresh_masked, axis=-1))
    cache_weights = jnp.where(cache_live, jnp.exp(cache_masked - maxima[..., None]), 0.0)
    fresh_weights = jnp.where(steps_live, jnp.exp(fresh_masked - maxima[..., None]), 0.0)
    totals = jnp.sum(cache_weights, axis=-1) + jnp.sum(fresh_weights, axis=-1)
    numerator = split_dot(cache_weights, cache_values, "tkgl,lkd->tkgd") + split_dot(
        fresh_weights, fresh_values, "tkgu,ukd->tkgd"
    )
    return (
        numerator.reshape(step_count, QH, HEAD_SIZE),
        maxima.reshape(step_count, QH),
        totals.reshape(step_count, QH),
    )


def per_device(queries, new_kv, suffix_kv, suffix_len, prefix_head, prefix_tail, prefix_len):
    team_count = lax.axis_size(("zl", "core"))
    prompt_row = lax.axis_index("prompt")
    team = lax.axis_index("zg")
    block_len = prefix_head.shape[1]
    step_count = queries.shape[2]
    rows_per_sample = step_count * GROUP

    moved_tail = shifted(prefix_tail, "prompt", -1)
    own_rows = queries[0, 0]
    partner_rows = shifted(own_rows, "zg", 1)

    def by_head(block):
        return block[0].reshape(block_len, 2, KVH, HEAD_SIZE).transpose(2, 1, 0, 3).reshape(KVH, 2 * block_len, HEAD_SIZE)

    def query_groups(rows):
        return rows.reshape(step_count, KVH, GROUP, HEAD_SIZE).transpose(1, 0, 2, 3).reshape(KVH, rows_per_sample, HEAD_SIZE)

    span = 2 * block_len
    first = lax.all_to_all(
        jnp.concatenate([by_head(prefix_head), query_groups(own_rows)], axis=1), ("zl", "core"), 0, 0, tiled=True
    )
    second = lax.all_to_all(
        jnp.concatenate([by_head(moved_tail), query_groups(partner_rows)], axis=1), ("zl", "core"), 0, 0, tiled=True
    )
    query_parts = jnp.stack([first[:, span:], second[:, span:]])
    query_parts = jnp.where(team == 0, query_parts, query_parts[::-1])
    query_matrix = query_parts.reshape(2 * team_count * rows_per_sample, HEAD_SIZE)

    member = jnp.arange(team_count, dtype=jnp.int32)[None, :, None]
    half = jnp.arange(2, dtype=jnp.int32)[:, None, None]
    offset = jnp.arange(block_len, dtype=jnp.int32)[None, None, :]
    prefix_half_len = block_len * team_count * 2
    positions = half * prefix_half_len + (team * team_count + member) * block_len + offset
    bias = jnp.where(positions.reshape(2, -1) < prefix_len[prompt_row], 0.0, NEG).astype(jnp.float32)
    sample_count = 2 * team_count
    outgoing_parts = prefix_attention(bias, query_matrix, first, second, block_len, rows_per_sample)
    returned = lax.all_to_all(outgoing_parts, ("zg", "zl", "core"), 0, 0, tiled=True)
    returned = returned.reshape(2, KVH, rows_per_sample + 2, HEAD_SIZE)
    lane_offset = (lax.axis_index(("zg", "zl", "core")) % (ROW_BLOCK // rows_per_sample)) * rows_per_sample

    def unpack(parts):
        numer = parts[:, :rows_per_sample].reshape(KVH, step_count, GROUP, HEAD_SIZE)
        numer = numer.transpose(1, 0, 2, 3).reshape(step_count, QH, HEAD_SIZE)
        maxi = lax.dynamic_slice_in_dim(parts[:, rows_per_sample], lane_offset, rows_per_sample, axis=1)
        maxi = maxi.reshape(KVH, step_count, GROUP)
        maxi = maxi.transpose(1, 0, 2).reshape(step_count, QH)
        tot = lax.dynamic_slice_in_dim(parts[:, rows_per_sample + 1], lane_offset, rows_per_sample, axis=1)
        tot = tot.reshape(KVH, step_count, GROUP)
        tot = tot.transpose(1, 0, 2).reshape(step_count, QH)
        return numer, maxi, tot

    first_numer, first_max, first_tot = unpack(returned[0])
    second_numer, second_max, second_tot = unpack(returned[1])
    near_numer, near_max, near_tot = suffix_terms(own_rows, suffix_kv[0, 0], new_kv[0, 0], suffix_len[0, 0])

    top = jnp.maximum(jnp.maximum(first_max, second_max), near_max)
    first_scale = jnp.exp(first_max - top)
    second_scale = jnp.exp(second_max - top)
    near_scale = jnp.exp(near_max - top)
    numer = (
        first_numer * first_scale[..., None]
        + second_numer * second_scale[..., None]
        + near_numer * near_scale[..., None]
    )
    total = first_tot * first_scale + second_tot * second_scale + near_tot * near_scale
    attended = (numer / total[..., None]).astype(jnp.bfloat16)
    return attended.reshape(queries.shape)


def solution(mesh):
    prompts, samples = mesh.devices.shape
    teams = 2
    team_mesh = jax.sharding.Mesh(
        mesh.devices.reshape(prompts, teams, samples // (2 * teams), 2), ("prompt", "zg", "zl", "core")
    )
    spread = ("zg", "zl", "core")
    in_specs = (
        P("prompt", spread, None, None),
        P("prompt", spread, None, None, None),
        P("prompt", spread, None, None, None),
        P("prompt", spread),
        P("prompt", spread, None, None),
        P("prompt", spread, None, None),
        P(),
    )
    out_specs = P("prompt", spread, None, None)
    return jax.shard_map(
        per_device, mesh=team_mesh, in_specs=in_specs, out_specs=out_specs, check_vma=False
    )
```

```python
import functools

import jax
import jax.numpy as jnp
from jax import lax
from jax.experimental import pallas as pl
from jax.sharding import PartitionSpec as P

QH = 64
KVH = 8
HEAD_SIZE = 128
GROUP = QH // KVH


NEG = -1e30
ROW_BLOCK = 128


def prefix_kernel(block, bias_ref, query_ref, first_ref, second_ref, out_ref):
    query = query_ref[...]
    members = first_ref.shape[0]
    parts = []
    for index, source in enumerate((first_ref, second_ref)):
        keys = source[:, :block, :].reshape(members * block, HEAD_SIZE)
        values = source[:, block : 2 * block, :].reshape(members * block, HEAD_SIZE)
        scores = lax.dot_general(
            query, keys, (((1,), (1,)), ((), ())), preferred_element_type=jnp.float32
        ) * HEAD_SIZE ** (-0.5) + bias_ref[index : index + 1, :]
        parts.append((scores, values))
    maxima = jnp.maximum(
        jnp.max(parts[0][0], axis=1, keepdims=True), jnp.max(parts[1][0], axis=1, keepdims=True)
    )
    numer = None
    totals = None
    for scores, values in parts:
        weights = jnp.exp(scores - maxima)
        part_total = jnp.sum(weights, axis=1, keepdims=True)
        high = weights.astype(jnp.bfloat16)
        low = (weights - high.astype(jnp.float32)).astype(jnp.bfloat16)
        part = jnp.dot(high, values, preferred_element_type=jnp.float32) + jnp.dot(
            low, values, preferred_element_type=jnp.float32
        )
        numer = part if numer is None else numer + part
        totals = part_total if totals is None else totals + part_total
    samples, rows, width = out_ref.shape
    rows = rows - 2
    out_ref[:, :rows, :] = numer.reshape(samples, rows, width)
    max_row = jnp.transpose(jnp.broadcast_to(maxima, (ROW_BLOCK, ROW_BLOCK)))[0:1, :]
    total_row = jnp.transpose(jnp.broadcast_to(totals, (ROW_BLOCK, ROW_BLOCK)))[0:1, :]
    out_ref[:, rows : rows + 1, :] = jnp.broadcast_to(max_row[None], (samples, 1, width))
    out_ref[:, rows + 1 : rows + 2, :] = jnp.broadcast_to(total_row[None], (samples, 1, width))


def prefix_attention(bias, query_matrix, first, second, block, rows_per_sample):
    rows, width = query_matrix.shape
    span = first.shape[0] * block
    per_block = ROW_BLOCK // rows_per_sample
    return pl.pallas_call(
        functools.partial(prefix_kernel, block),
        grid=(rows // ROW_BLOCK,),
        in_specs=[
            pl.BlockSpec(bias.shape, lambda i: (0, 0)),
            pl.BlockSpec((ROW_BLOCK, width), lambda i: (i, 0)),
            pl.BlockSpec(first.shape, lambda i: (0, 0, 0)),
            pl.BlockSpec(second.shape, lambda i: (0, 0, 0)),
        ],
        out_specs=pl.BlockSpec((per_block, rows_per_sample + 2, width), lambda i: (i, 0, 0)),
        out_shape=jax.ShapeDtypeStruct((rows // rows_per_sample, rows_per_sample + 2, width), jnp.float32),
        cost_estimate=pl.CostEstimate(
            flops=3 * rows * span * width, transcendentals=rows * span // 2, bytes_accessed=2 * (rows + span) * width + 4 * rows * width
        ),
    )(bias, query_matrix, first, second)


def shifted(value, axis, steps):
    count = lax.axis_size(axis)
    pairs = [(source, (source + steps) % count) for source in range(count)]
    return lax.ppermute(value, axis, pairs)


def split_dot(weights, value_matrix, form):
    rounded = lax.reduce_precision(weights, exponent_bits=8, mantissa_bits=7)
    high = rounded.astype(jnp.bfloat16)
    low = (weights - rounded).astype(jnp.bfloat16)
    return jnp.einsum(form, high, value_matrix, preferred_element_type=jnp.float32) + jnp.einsum(
        form, low, value_matrix, preferred_element_type=jnp.float32
    )


def suffix_terms(query_rows, cache, fresh, length):
    step_count = query_rows.shape[0]
    slots = cache.shape[0]
    grouped = query_rows.reshape(step_count, KVH, GROUP, HEAD_SIZE)
    cache_keys = cache[:, 0].reshape(slots, KVH, HEAD_SIZE)
    cache_values = cache[:, 1].reshape(slots, KVH, HEAD_SIZE)
    fresh_keys = fresh[:, 0].reshape(step_count, KVH, HEAD_SIZE)
    fresh_values = fresh[:, 1].reshape(step_count, KVH, HEAD_SIZE)
    scale = HEAD_SIZE ** (-0.5)
    cache_scores = jnp.einsum("tkgd,lkd->tkgl", grouped, cache_keys, preferred_element_type=jnp.float32) * scale
    fresh_scores = jnp.einsum("tkgd,ukd->tkgu", grouped, fresh_keys, preferred_element_type=jnp.float32) * scale
    cache_live = (jnp.arange(slots, dtype=jnp.int32) < length)[None, None, None, :]
    steps_live = (
        jnp.arange(step_count, dtype=jnp.int32)[None, :] <= jnp.arange(step_count, dtype=jnp.int32)[:, None]
    )[:, None, None, :]
    cache_masked = jnp.where(cache_live, cache_scores, NEG)
    fresh_masked = jnp.where(steps_live, fresh_scores, NEG)
    maxima = jnp.maximum(jnp.max(cache_masked, axis=-1), jnp.max(fresh_masked, axis=-1))
    cache_weights = jnp.where(cache_live, jnp.exp(cache_masked - maxima[..., None]), 0.0)
    fresh_weights = jnp.where(steps_live, jnp.exp(fresh_masked - maxima[..., None]), 0.0)
    totals = jnp.sum(cache_weights, axis=-1) + jnp.sum(fresh_weights, axis=-1)
    numerator = split_dot(cache_weights, cache_values, "tkgl,lkd->tkgd") + split_dot(
        fresh_weights, fresh_values, "tkgu,ukd->tkgd"
    )
    return (
        numerator.reshape(step_count, QH, HEAD_SIZE),
        maxima.reshape(step_count, QH),
        totals.reshape(step_count, QH),
    )


def per_device(queries, new_kv, suffix_kv, suffix_len, prefix_head, prefix_tail, prefix_len):
    team_count = lax.axis_size(("zl", "core"))
    prompt_row = lax.axis_index("prompt")
    team = lax.axis_index("zg")
    block_len = prefix_head.shape[1]
    step_count = queries.shape[2]
    rows_per_sample = step_count * GROUP

    own_rows = queries[0, 0]

    def by_head(block):
        return block[0].reshape(block_len, 2, KVH, HEAD_SIZE).transpose(2, 1, 0, 3).reshape(KVH, 2 * block_len, HEAD_SIZE)

    def query_groups(rows):
        return rows.reshape(step_count, KVH, GROUP, HEAD_SIZE).transpose(1, 0, 2, 3).reshape(KVH, rows_per_sample, HEAD_SIZE)

    moved_tail = shifted(by_head(prefix_tail), "prompt", -1)
    span = 2 * block_len
    first = lax.all_to_all(
        jnp.concatenate([by_head(prefix_head), query_groups(own_rows)], axis=1), ("zl", "core"), 0, 0, tiled=True
    )
    second = lax.all_to_all(moved_tail, ("zl", "core"), 0, 0, tiled=True)
    team_queries = first[:, span:]
    partner_queries = shifted(team_queries, "zg", 1)
    query_parts = jnp.stack([team_queries, partner_queries])
    query_parts = jnp.where(team == 0, query_parts, query_parts[::-1])
    query_matrix = query_parts.reshape(2 * team_count * rows_per_sample, HEAD_SIZE)

    member = jnp.arange(team_count, dtype=jnp.int32)[None, :, None]
    half = jnp.arange(2, dtype=jnp.int32)[:, None, None]
    offset = jnp.arange(block_len, dtype=jnp.int32)[None, None, :]
    prefix_half_len = block_len * team_count * 2
    positions = half * prefix_half_len + (team * team_count + member) * block_len + offset
    bias = jnp.where(positions.reshape(2, -1) < prefix_len[prompt_row], 0.0, NEG).astype(jnp.float32)
    sample_count = 2 * team_count
    outgoing_parts = prefix_attention(bias, query_matrix, first, second, block_len, rows_per_sample)
    returned = lax.all_to_all(outgoing_parts, ("zg", "zl", "core"), 0, 0, tiled=True)
    returned = returned.reshape(2, KVH, rows_per_sample + 2, HEAD_SIZE)
    lane_offset = (lax.axis_index(("zg", "zl", "core")) % (ROW_BLOCK // rows_per_sample)) * rows_per_sample

    def unpack(parts):
        numer = parts[:, :rows_per_sample].reshape(KVH, step_count, GROUP, HEAD_SIZE)
        numer = numer.transpose(1, 0, 2, 3).reshape(step_count, QH, HEAD_SIZE)
        maxi = lax.dynamic_slice_in_dim(parts[:, rows_per_sample], lane_offset, rows_per_sample, axis=1)
        maxi = maxi.reshape(KVH, step_count, GROUP)
        maxi = maxi.transpose(1, 0, 2).reshape(step_count, QH)
        tot = lax.dynamic_slice_in_dim(parts[:, rows_per_sample + 1], lane_offset, rows_per_sample, axis=1)
        tot = tot.reshape(KVH, step_count, GROUP)
        tot = tot.transpose(1, 0, 2).reshape(step_count, QH)
        return numer, maxi, tot

    first_numer, first_max, first_tot = unpack(returned[0])
    second_numer, second_max, second_tot = unpack(returned[1])
    near_numer, near_max, near_tot = suffix_terms(own_rows, suffix_kv[0, 0], new_kv[0, 0], suffix_len[0, 0])

    top = jnp.maximum(jnp.maximum(first_max, second_max), near_max)
    first_scale = jnp.exp(first_max - top)
    second_scale = jnp.exp(second_max - top)
    near_scale = jnp.exp(near_max - top)
    numer = (
        first_numer * first_scale[..., None]
        + second_numer * second_scale[..., None]
        + near_numer * near_scale[..., None]
    )
    total = first_tot * first_scale + second_tot * second_scale + near_tot * near_scale
    attended = (numer / total[..., None]).astype(jnp.bfloat16)
    return attended.reshape(queries.shape)


def solution(mesh):
    prompts, samples = mesh.devices.shape
    teams = 2
    team_mesh = jax.sharding.Mesh(
        mesh.devices.reshape(prompts, teams, samples // (2 * teams), 2), ("prompt", "zg", "zl", "core")
    )
    spread = ("zg", "zl", "core")
    in_specs = (
        P("prompt", spread, None, None),
        P("prompt", spread, None, None, None),
        P("prompt", spread, None, None, None),
        P("prompt", spread),
        P("prompt", spread, None, None),
        P("prompt", spread, None, None),
        P(),
    )
    out_specs = P("prompt", spread, None, None)
    return jax.shard_map(
        per_device, mesh=team_mesh, in_specs=in_specs, out_specs=out_specs, check_vma=False
    )
```

```python
import functools

import jax
import jax.numpy as jnp
from jax import lax
from jax.experimental import pallas as pl
from jax.sharding import PartitionSpec as P

QH = 64
KVH = 8
HEAD_SIZE = 128
GROUP = QH // KVH


NEG = -1e30
ROW_BLOCK = 128


def prefix_kernel(block, bias_ref, query_ref, first_ref, second_ref, out_ref):
    query = query_ref[...]
    members = first_ref.shape[0]
    parts = []
    for index, source in enumerate((first_ref, second_ref)):
        keys = source[:, :block, :].reshape(members * block, HEAD_SIZE)
        values = source[:, block : 2 * block, :].reshape(members * block, HEAD_SIZE)
        scores = lax.dot_general(
            query, keys, (((1,), (1,)), ((), ())), preferred_element_type=jnp.float32
        ) * HEAD_SIZE ** (-0.5) + bias_ref[index : index + 1, :]
        parts.append((scores, values))
    maxima = jnp.maximum(
        jnp.max(parts[0][0], axis=1, keepdims=True), jnp.max(parts[1][0], axis=1, keepdims=True)
    )
    numer = None
    totals = None
    for scores, values in parts:
        weights = jnp.exp(scores - maxima)
        part_total = jnp.sum(weights, axis=1, keepdims=True)
        high = weights.astype(jnp.bfloat16)
        low = (weights - high.astype(jnp.float32)).astype(jnp.bfloat16)
        part = jnp.dot(high, values, preferred_element_type=jnp.float32) + jnp.dot(
            low, values, preferred_element_type=jnp.float32
        )
        numer = part if numer is None else numer + part
        totals = part_total if totals is None else totals + part_total
    samples, rows, width = out_ref.shape
    rows = rows - 2
    out_ref[:, :rows, :] = numer.reshape(samples, rows, width)
    max_row = jnp.transpose(jnp.broadcast_to(maxima, (ROW_BLOCK, ROW_BLOCK)))[0:1, :]
    total_row = jnp.transpose(jnp.broadcast_to(totals, (ROW_BLOCK, ROW_BLOCK)))[0:1, :]
    out_ref[:, rows : rows + 1, :] = jnp.broadcast_to(max_row[None], (samples, 1, width))
    out_ref[:, rows + 1 : rows + 2, :] = jnp.broadcast_to(total_row[None], (samples, 1, width))


def prefix_attention(bias, query_matrix, first, second, block, rows_per_sample):
    rows, width = query_matrix.shape
    span = first.shape[0] * block
    per_block = ROW_BLOCK // rows_per_sample
    return pl.pallas_call(
        functools.partial(prefix_kernel, block),
        grid=(rows // ROW_BLOCK,),
        in_specs=[
            pl.BlockSpec(bias.shape, lambda i: (0, 0)),
            pl.BlockSpec((ROW_BLOCK, width), lambda i: (i, 0)),
            pl.BlockSpec(first.shape, lambda i: (0, 0, 0)),
            pl.BlockSpec(second.shape, lambda i: (0, 0, 0)),
        ],
        out_specs=pl.BlockSpec((per_block, rows_per_sample + 2, width), lambda i: (i, 0, 0)),
        out_shape=jax.ShapeDtypeStruct((rows // rows_per_sample, rows_per_sample + 2, width), jnp.float32),
        cost_estimate=pl.CostEstimate(
            flops=3 * rows * span * width, transcendentals=rows * span // 2, bytes_accessed=2 * (rows + span) * width + 4 * rows * width
        ),
    )(bias, query_matrix, first, second)


def shifted(value, axis, steps):
    count = lax.axis_size(axis)
    pairs = [(source, (source + steps) % count) for source in range(count)]
    return lax.ppermute(value, axis, pairs)


def split_dot(weights, value_matrix, form):
    rounded = lax.reduce_precision(weights, exponent_bits=8, mantissa_bits=7)
    high = rounded.astype(jnp.bfloat16)
    low = (weights - rounded).astype(jnp.bfloat16)
    return jnp.einsum(form, high, value_matrix, preferred_element_type=jnp.float32) + jnp.einsum(
        form, low, value_matrix, preferred_element_type=jnp.float32
    )


def suffix_terms(query_rows, cache, fresh, length):
    step_count = query_rows.shape[0]
    slots = cache.shape[0]
    grouped = query_rows.reshape(step_count, KVH, GROUP, HEAD_SIZE)
    cache_keys = cache[:, 0].reshape(slots, KVH, HEAD_SIZE)
    cache_values = cache[:, 1].reshape(slots, KVH, HEAD_SIZE)
    fresh_keys = fresh[:, 0].reshape(step_count, KVH, HEAD_SIZE)
    fresh_values = fresh[:, 1].reshape(step_count, KVH, HEAD_SIZE)
    scale = HEAD_SIZE ** (-0.5)
    cache_scores = jnp.einsum("tkgd,lkd->tkgl", grouped, cache_keys, preferred_element_type=jnp.float32) * scale
    fresh_scores = jnp.einsum("tkgd,ukd->tkgu", grouped, fresh_keys, preferred_element_type=jnp.float32) * scale
    cache_live = (jnp.arange(slots, dtype=jnp.int32) < length)[None, None, None, :]
    steps_live = (
        jnp.arange(step_count, dtype=jnp.int32)[None, :] <= jnp.arange(step_count, dtype=jnp.int32)[:, None]
    )[:, None, None, :]
    cache_masked = jnp.where(cache_live, cache_scores, NEG)
    fresh_masked = jnp.where(steps_live, fresh_scores, NEG)
    maxima = jnp.maximum(jnp.max(cache_masked, axis=-1), jnp.max(fresh_masked, axis=-1))
    cache_weights = jnp.where(cache_live, jnp.exp(cache_masked - maxima[..., None]), 0.0)
    fresh_weights = jnp.where(steps_live, jnp.exp(fresh_masked - maxima[..., None]), 0.0)
    totals = jnp.sum(cache_weights, axis=-1) + jnp.sum(fresh_weights, axis=-1)
    numerator = split_dot(cache_weights, cache_values, "tkgl,lkd->tkgd") + split_dot(
        fresh_weights, fresh_values, "tkgu,ukd->tkgd"
    )
    return (
        numerator.reshape(step_count, QH, HEAD_SIZE),
        maxima.reshape(step_count, QH),
        totals.reshape(step_count, QH),
    )


def per_device(queries, new_kv, suffix_kv, suffix_len, prefix_head, prefix_tail, prefix_len):
    team_count = lax.axis_size(("zl", "core"))
    prompt_row = lax.axis_index("prompt")
    team = lax.axis_index("zg")
    block_len = prefix_head.shape[1]
    step_count = queries.shape[2]
    rows_per_sample = step_count * GROUP

    own_rows = queries[0, 0]
    partner_rows = shifted(own_rows, "zg", 1)

    def by_head(block):
        return block[0].reshape(block_len, 2, KVH, HEAD_SIZE).transpose(2, 1, 0, 3).reshape(KVH, 2 * block_len, HEAD_SIZE)

    def query_groups(rows):
        return rows.reshape(step_count, KVH, GROUP, HEAD_SIZE).transpose(1, 0, 2, 3).reshape(KVH, rows_per_sample, HEAD_SIZE)

    moved_tail = shifted(by_head(prefix_tail), "prompt", -1)
    span = 2 * block_len
    first = lax.all_to_all(
        jnp.concatenate([by_head(prefix_head), query_groups(own_rows)], axis=1), ("zl", "core"), 0, 0, tiled=True
    )
    second = lax.all_to_all(
        jnp.concatenate([moved_tail, query_groups(partner_rows)], axis=1), ("zl", "core"), 0, 0, tiled=True
    )
    query_parts = jnp.stack([first[:, span:], second[:, span:]])
    query_parts = jnp.where(team == 0, query_parts, query_parts[::-1])
    query_matrix = query_parts.reshape(2 * team_count * rows_per_sample, HEAD_SIZE)

    member = jnp.arange(team_count, dtype=jnp.int32)[None, :, None]
    half = jnp.arange(2, dtype=jnp.int32)[:, None, None]
    offset = jnp.arange(block_len, dtype=jnp.int32)[None, None, :]
    prefix_half_len = block_len * team_count * 2
    positions = half * prefix_half_len + (team * team_count + member) * block_len + offset
    bias = jnp.where(positions.reshape(2, -1) < prefix_len[prompt_row], 0.0, NEG).astype(jnp.float32)
    sample_count = 2 * team_count
    outgoing_parts = prefix_attention(bias, query_matrix, first, second, block_len, rows_per_sample)
    returned = lax.all_to_all(outgoing_parts, ("zg", "zl", "core"), 0, 0, tiled=True)
    returned = returned.reshape(2, KVH, rows_per_sample + 2, HEAD_SIZE)
    lane_offset = (lax.axis_index(("zg", "zl", "core")) % (ROW_BLOCK // rows_per_sample)) * rows_per_sample

    def unpack(parts):
        numer = parts[:, :rows_per_sample].reshape(KVH, step_count, GROUP, HEAD_SIZE)
        numer = numer.transpose(1, 0, 2, 3).reshape(step_count, QH, HEAD_SIZE)
        maxi = lax.dynamic_slice_in_dim(parts[:, rows_per_sample], lane_offset, rows_per_sample, axis=1)
        maxi = maxi.reshape(KVH, step_count, GROUP)
        maxi = maxi.transpose(1, 0, 2).reshape(step_count, QH)
        tot = lax.dynamic_slice_in_dim(parts[:, rows_per_sample + 1], lane_offset, rows_per_sample, axis=1)
        tot = tot.reshape(KVH, step_count, GROUP)
        tot = tot.transpose(1, 0, 2).reshape(step_count, QH)
        return numer, maxi, tot

    first_numer, first_max, first_tot = unpack(returned[0])
    second_numer, second_max, second_tot = unpack(returned[1])
    near_numer, near_max, near_tot = suffix_terms(own_rows, suffix_kv[0, 0], new_kv[0, 0], suffix_len[0, 0])

    top = jnp.maximum(jnp.maximum(first_max, second_max), near_max)
    first_scale = jnp.exp(first_max - top)
    second_scale = jnp.exp(second_max - top)
    near_scale = jnp.exp(near_max - top)
    numer = (
        first_numer * first_scale[..., None]
        + second_numer * second_scale[..., None]
        + near_numer * near_scale[..., None]
    )
    total = first_tot * first_scale + second_tot * second_scale + near_tot * near_scale
    attended = (numer / total[..., None]).astype(jnp.bfloat16)
    return attended.reshape(queries.shape)


def solution(mesh):
    prompts, samples = mesh.devices.shape
    teams = 2
    team_mesh = jax.sharding.Mesh(
        mesh.devices.reshape(prompts, teams, samples // (2 * teams), 2), ("prompt", "zg", "zl", "core")
    )
    spread = ("zg", "zl", "core")
    in_specs = (
        P("prompt", spread, None, None),
        P("prompt", spread, None, None, None),
        P("prompt", spread, None, None, None),
        P("prompt", spread),
        P("prompt", spread, None, None),
        P("prompt", spread, None, None),
        P(),
    )
    out_specs = P("prompt", spread, None, None)
    return jax.shard_map(
        per_device, mesh=team_mesh, in_specs=in_specs, out_specs=out_specs, check_vma=False
    )
```

```python
import functools

import jax
import jax.numpy as jnp
from jax import lax
from jax.experimental import pallas as pl
from jax.experimental.pallas import tpu as pltpu
from jax.sharding import PartitionSpec as P

QH = 64
KVH = 8
HEAD_SIZE = 128
GROUP = QH // KVH


NEG = -1e30
ROW_BLOCK = 128


def prefix_kernel(block, team_ref, bias_ref, first_ref, second_ref, out_ref):
    samples, rows, width = out_ref.shape
    rows = rows - 2
    members = first_ref.shape[0]
    blocks_per_team = members // samples
    index = pl.program_id(0)
    start = (index % blocks_per_team) * samples
    from_first = index // blocks_per_team == team_ref[0]
    first_rows = first_ref[pl.ds(start, samples), 2 * block :, :]
    second_rows = second_ref[pl.ds(start, samples), 2 * block :, :]
    query = jnp.where(from_first, first_rows, second_rows).reshape(samples * rows, width)
    parts = []
    for which, source in enumerate((first_ref, second_ref)):
        keys = source[:, :block, :].reshape(members * block, HEAD_SIZE)
        values = source[:, block : 2 * block, :].reshape(members * block, HEAD_SIZE)
        scores = lax.dot_general(
            query, keys, (((1,), (1,)), ((), ())), preferred_element_type=jnp.float32
        ) * HEAD_SIZE ** (-0.5) + bias_ref[which : which + 1, :]
        parts.append((scores, values))
    maxima = jnp.maximum(
        jnp.max(parts[0][0], axis=1, keepdims=True), jnp.max(parts[1][0], axis=1, keepdims=True)
    )
    numer = None
    totals = None
    for scores, values in parts:
        weights = jnp.exp(scores - maxima)
        part_total = jnp.sum(weights, axis=1, keepdims=True)
        high = weights.astype(jnp.bfloat16)
        low = (weights - high.astype(jnp.float32)).astype(jnp.bfloat16)
        part = jnp.dot(high, values, preferred_element_type=jnp.float32) + jnp.dot(
            low, values, preferred_element_type=jnp.float32
        )
        numer = part if numer is None else numer + part
        totals = part_total if totals is None else totals + part_total
    out_ref[:, :rows, :] = numer.reshape(samples, rows, width)
    max_row = jnp.transpose(jnp.broadcast_to(maxima, (ROW_BLOCK, ROW_BLOCK)))[0:1, :]
    total_row = jnp.transpose(jnp.broadcast_to(totals, (ROW_BLOCK, ROW_BLOCK)))[0:1, :]
    out_ref[:, rows : rows + 1, :] = jnp.broadcast_to(max_row[None], (samples, 1, width))
    out_ref[:, rows + 1 : rows + 2, :] = jnp.broadcast_to(total_row[None], (samples, 1, width))


def prefix_attention(team, bias, first, second, block, rows_per_sample):
    width = first.shape[2]
    rows = 2 * first.shape[0] * rows_per_sample
    span = first.shape[0] * block
    per_block = ROW_BLOCK // rows_per_sample
    return pl.pallas_call(
        functools.partial(prefix_kernel, block),
        grid=(rows // ROW_BLOCK,),
        in_specs=[
            pl.BlockSpec(memory_space=pltpu.SMEM),
            pl.BlockSpec(bias.shape, lambda i: (0, 0)),
            pl.BlockSpec(first.shape, lambda i: (0, 0, 0)),
            pl.BlockSpec(second.shape, lambda i: (0, 0, 0)),
        ],
        out_specs=pl.BlockSpec((per_block, rows_per_sample + 2, width), lambda i: (i, 0, 0)),
        out_shape=jax.ShapeDtypeStruct((rows // rows_per_sample, rows_per_sample + 2, width), jnp.float32),
        cost_estimate=pl.CostEstimate(
            flops=3 * rows * span * width, transcendentals=rows * span // 2, bytes_accessed=2 * (rows + span) * width + 4 * rows * width
        ),
    )(team, bias, first, second)


def shifted(value, axis, steps):
    count = lax.axis_size(axis)
    pairs = [(source, (source + steps) % count) for source in range(count)]
    return lax.ppermute(value, axis, pairs)


def split_dot(weights, value_matrix, form):
    rounded = lax.reduce_precision(weights, exponent_bits=8, mantissa_bits=7)
    high = rounded.astype(jnp.bfloat16)
    low = (weights - rounded).astype(jnp.bfloat16)
    return jnp.einsum(form, high, value_matrix, preferred_element_type=jnp.float32) + jnp.einsum(
        form, low, value_matrix, preferred_element_type=jnp.float32
    )


def suffix_terms(query_rows, cache, fresh, length):
    step_count = query_rows.shape[0]
    slots = cache.shape[0]
    grouped = query_rows.reshape(step_count, KVH, GROUP, HEAD_SIZE)
    cache_keys = cache[:, 0].reshape(slots, KVH, HEAD_SIZE)
    cache_values = cache[:, 1].reshape(slots, KVH, HEAD_SIZE)
    fresh_keys = fresh[:, 0].reshape(step_count, KVH, HEAD_SIZE)
    fresh_values = fresh[:, 1].reshape(step_count, KVH, HEAD_SIZE)
    scale = HEAD_SIZE ** (-0.5)
    cache_scores = jnp.einsum("tkgd,lkd->tkgl", grouped, cache_keys, preferred_element_type=jnp.float32) * scale
    fresh_scores = jnp.einsum("tkgd,ukd->tkgu", grouped, fresh_keys, preferred_element_type=jnp.float32) * scale
    cache_live = (jnp.arange(slots, dtype=jnp.int32) < length)[None, None, None, :]
    steps_live = (
        jnp.arange(step_count, dtype=jnp.int32)[None, :] <= jnp.arange(step_count, dtype=jnp.int32)[:, None]
    )[:, None, None, :]
    cache_masked = jnp.where(cache_live, cache_scores, NEG)
    fresh_masked = jnp.where(steps_live, fresh_scores, NEG)
    maxima = jnp.maximum(jnp.max(cache_masked, axis=-1), jnp.max(fresh_masked, axis=-1))
    cache_weights = jnp.where(cache_live, jnp.exp(cache_masked - maxima[..., None]), 0.0)
    fresh_weights = jnp.where(steps_live, jnp.exp(fresh_masked - maxima[..., None]), 0.0)
    totals = jnp.sum(cache_weights, axis=-1) + jnp.sum(fresh_weights, axis=-1)
    numerator = split_dot(cache_weights, cache_values, "tkgl,lkd->tkgd") + split_dot(
        fresh_weights, fresh_values, "tkgu,ukd->tkgd"
    )
    return (
        numerator.reshape(step_count, QH, HEAD_SIZE),
        maxima.reshape(step_count, QH),
        totals.reshape(step_count, QH),
    )


def per_device(queries, new_kv, suffix_kv, suffix_len, prefix_head, prefix_tail, prefix_len):
    team_count = lax.axis_size(("zl", "core"))
    prompt_row = lax.axis_index("prompt")
    team = lax.axis_index("zg")
    block_len = prefix_head.shape[1]
    step_count = queries.shape[2]
    rows_per_sample = step_count * GROUP

    moved_tail = shifted(prefix_tail, "prompt", -1)
    own_rows = queries[0, 0]
    partner_rows = shifted(own_rows, "zg", 1)

    def by_head(block):
        return block[0].reshape(block_len, 2, KVH, HEAD_SIZE).transpose(2, 1, 0, 3).reshape(KVH, 2 * block_len, HEAD_SIZE)

    def query_groups(rows):
        return rows.reshape(step_count, KVH, GROUP, HEAD_SIZE).transpose(1, 0, 2, 3).reshape(KVH, rows_per_sample, HEAD_SIZE)

    span = 2 * block_len
    first = lax.all_to_all(
        jnp.concatenate([by_head(prefix_head), query_groups(own_rows)], axis=1), ("zl", "core"), 0, 0, tiled=True
    )
    second = lax.all_to_all(
        jnp.concatenate([by_head(moved_tail), query_groups(partner_rows)], axis=1), ("zl", "core"), 0, 0, tiled=True
    )

    member = jnp.arange(team_count, dtype=jnp.int32)[None, :, None]
    half = jnp.arange(2, dtype=jnp.int32)[:, None, None]
    offset = jnp.arange(block_len, dtype=jnp.int32)[None, None, :]
    prefix_half_len = block_len * team_count * 2
    positions = half * prefix_half_len + (team * team_count + member) * block_len + offset
    bias = jnp.where(positions.reshape(2, -1) < prefix_len[prompt_row], 0.0, NEG).astype(jnp.float32)
    sample_count = 2 * team_count
    outgoing_parts = prefix_attention(team.reshape(1), bias, first, second, block_len, rows_per_sample)
    returned = lax.all_to_all(outgoing_parts, ("zg", "zl", "core"), 0, 0, tiled=True)
    returned = returned.reshape(2, KVH, rows_per_sample + 2, HEAD_SIZE)
    lane_offset = (lax.axis_index(("zg", "zl", "core")) % (ROW_BLOCK // rows_per_sample)) * rows_per_sample

    def unpack(parts):
        numer = parts[:, :rows_per_sample].reshape(KVH, step_count, GROUP, HEAD_SIZE)
        numer = numer.transpose(1, 0, 2, 3).reshape(step_count, QH, HEAD_SIZE)
        maxi = lax.dynamic_slice_in_dim(parts[:, rows_per_sample], lane_offset, rows_per_sample, axis=1)
        maxi = maxi.reshape(KVH, step_count, GROUP)
        maxi = maxi.transpose(1, 0, 2).reshape(step_count, QH)
        tot = lax.dynamic_slice_in_dim(parts[:, rows_per_sample + 1], lane_offset, rows_per_sample, axis=1)
        tot = tot.reshape(KVH, step_count, GROUP)
        tot = tot.transpose(1, 0, 2).reshape(step_count, QH)
        return numer, maxi, tot

    first_numer, first_max, first_tot = unpack(returned[0])
    second_numer, second_max, second_tot = unpack(returned[1])
    near_numer, near_max, near_tot = suffix_terms(own_rows, suffix_kv[0, 0], new_kv[0, 0], suffix_len[0, 0])

    top = jnp.maximum(jnp.maximum(first_max, second_max), near_max)
    first_scale = jnp.exp(first_max - top)
    second_scale = jnp.exp(second_max - top)
    near_scale = jnp.exp(near_max - top)
    numer = (
        first_numer * first_scale[..., None]
        + second_numer * second_scale[..., None]
        + near_numer * near_scale[..., None]
    )
    total = first_tot * first_scale + second_tot * second_scale + near_tot * near_scale
    attended = (numer / total[..., None]).astype(jnp.bfloat16)
    return attended.reshape(queries.shape)


def solution(mesh):
    prompts, samples = mesh.devices.shape
    teams = 2
    team_mesh = jax.sharding.Mesh(
        mesh.devices.reshape(prompts, teams, samples // (2 * teams), 2), ("prompt", "zg", "zl", "core")
    )
    spread = ("zg", "zl", "core")
    in_specs = (
        P("prompt", spread, None, None),
        P("prompt", spread, None, None, None),
        P("prompt", spread, None, None, None),
        P("prompt", spread),
        P("prompt", spread, None, None),
        P("prompt", spread, None, None),
        P(),
    )
    out_specs = P("prompt", spread, None, None)
    return jax.shard_map(
        per_device, mesh=team_mesh, in_specs=in_specs, out_specs=out_specs, check_vma=False
    )
```

```python
import functools

import jax
import jax.numpy as jnp
from jax import lax
from jax.experimental import pallas as pl
from jax.sharding import PartitionSpec as P

QH = 64
KVH = 8
HEAD_SIZE = 128
GROUP = QH // KVH


NEG = -1e30
ROW_BLOCK = 128


def prefix_kernel(block, bias_ref, query_ref, first_ref, second_ref, out_ref):
    query = query_ref[...]
    members = first_ref.shape[0]
    parts = []
    for index, source in enumerate((first_ref, second_ref)):
        keys = source[:, :block, :].reshape(members * block, HEAD_SIZE)
        values = source[:, block : 2 * block, :].reshape(members * block, HEAD_SIZE)
        scores = lax.dot_general(
            query, keys, (((1,), (1,)), ((), ())), preferred_element_type=jnp.float32
        ) * HEAD_SIZE ** (-0.5) + bias_ref[index : index + 1, :]
        parts.append((scores, values))
    maxima = jnp.maximum(
        jnp.max(parts[0][0], axis=1, keepdims=True), jnp.max(parts[1][0], axis=1, keepdims=True)
    )
    numer = None
    totals = None
    for scores, values in parts:
        weights = jnp.exp(scores - maxima)
        part_total = jnp.sum(weights, axis=1, keepdims=True)
        high = weights.astype(jnp.bfloat16)
        low = (weights - high.astype(jnp.float32)).astype(jnp.bfloat16)
        part = jnp.dot(high, values, preferred_element_type=jnp.float32) + jnp.dot(
            low, values, preferred_element_type=jnp.float32
        )
        numer = part if numer is None else numer + part
        totals = part_total if totals is None else totals + part_total
    samples, rows, width = out_ref.shape
    rows = rows - 2
    out_ref[:, :rows, :] = numer.reshape(samples, rows, width)
    max_row = jnp.transpose(jnp.broadcast_to(maxima, (ROW_BLOCK, ROW_BLOCK)))[0:1, :]
    total_row = jnp.transpose(jnp.broadcast_to(totals, (ROW_BLOCK, ROW_BLOCK)))[0:1, :]
    out_ref[:, rows : rows + 1, :] = jnp.broadcast_to(max_row[None], (samples, 1, width))
    out_ref[:, rows + 1 : rows + 2, :] = jnp.broadcast_to(total_row[None], (samples, 1, width))


def prefix_attention(bias, query_matrix, first, second, block, rows_per_sample):
    rows, width = query_matrix.shape
    span = first.shape[0] * block
    per_block = ROW_BLOCK // rows_per_sample
    return pl.pallas_call(
        functools.partial(prefix_kernel, block),
        grid=(rows // ROW_BLOCK,),
        in_specs=[
            pl.BlockSpec(bias.shape, lambda i: (0, 0)),
            pl.BlockSpec((ROW_BLOCK, width), lambda i: (i, 0)),
            pl.BlockSpec(first.shape, lambda i: (0, 0, 0)),
            pl.BlockSpec(second.shape, lambda i: (0, 0, 0)),
        ],
        out_specs=pl.BlockSpec((per_block, rows_per_sample + 2, width), lambda i: (i, 0, 0)),
        out_shape=jax.ShapeDtypeStruct((rows // rows_per_sample, rows_per_sample + 2, width), jnp.float32),
        cost_estimate=pl.CostEstimate(
            flops=3 * rows * span * width, transcendentals=rows * span // 2, bytes_accessed=2 * (rows + span) * width + 4 * rows * width
        ),
    )(bias, query_matrix, first, second)


def shifted(value, axis, steps):
    count = lax.axis_size(axis)
    pairs = [(source, (source + steps) % count) for source in range(count)]
    return lax.ppermute(value, axis, pairs)


def split_dot(weights, value_matrix, form):
    rounded = lax.reduce_precision(weights, exponent_bits=8, mantissa_bits=7)
    high = rounded.astype(jnp.bfloat16)
    low = (weights - rounded).astype(jnp.bfloat16)
    return jnp.einsum(form, high, value_matrix, preferred_element_type=jnp.float32) + jnp.einsum(
        form, low, value_matrix, preferred_element_type=jnp.float32
    )


def suffix_terms(query_rows, cache, fresh, length):
    step_count = query_rows.shape[0]
    slots = cache.shape[0]
    grouped = query_rows.reshape(step_count, KVH, GROUP, HEAD_SIZE)
    cache_keys = cache[:, 0].reshape(slots, KVH, HEAD_SIZE)
    cache_values = cache[:, 1].reshape(slots, KVH, HEAD_SIZE)
    fresh_keys = fresh[:, 0].reshape(step_count, KVH, HEAD_SIZE)
    fresh_values = fresh[:, 1].reshape(step_count, KVH, HEAD_SIZE)
    scale = HEAD_SIZE ** (-0.5)
    cache_scores = jnp.einsum("tkgd,lkd->tkgl", grouped, cache_keys, preferred_element_type=jnp.float32) * scale
    fresh_scores = jnp.einsum("tkgd,ukd->tkgu", grouped, fresh_keys, preferred_element_type=jnp.float32) * scale
    cache_live = (jnp.arange(slots, dtype=jnp.int32) < length)[None, None, None, :]
    steps_live = (
        jnp.arange(step_count, dtype=jnp.int32)[None, :] <= jnp.arange(step_count, dtype=jnp.int32)[:, None]
    )[:, None, None, :]
    cache_masked = jnp.where(cache_live, cache_scores, NEG)
    fresh_masked = jnp.where(steps_live, fresh_scores, NEG)
    maxima = jnp.maximum(jnp.max(cache_masked, axis=-1), jnp.max(fresh_masked, axis=-1))
    cache_weights = jnp.where(cache_live, jnp.exp(cache_masked - maxima[..., None]), 0.0)
    fresh_weights = jnp.where(steps_live, jnp.exp(fresh_masked - maxima[..., None]), 0.0)
    totals = jnp.sum(cache_weights, axis=-1) + jnp.sum(fresh_weights, axis=-1)
    numerator = split_dot(cache_weights, cache_values, "tkgl,lkd->tkgd") + split_dot(
        fresh_weights, fresh_values, "tkgu,ukd->tkgd"
    )
    return (
        numerator.reshape(step_count, QH, HEAD_SIZE),
        maxima.reshape(step_count, QH),
        totals.reshape(step_count, QH),
    )


def per_device(queries, new_kv, suffix_kv, suffix_len, prefix_head, prefix_tail, prefix_len):
    team_count = lax.axis_size(("zl", "core"))
    prompt_row = lax.axis_index("prompt")
    team = lax.axis_index("zg")
    block_len = prefix_head.shape[1]
    step_count = queries.shape[2]
    rows_per_sample = step_count * GROUP

    moved_tail = shifted(prefix_tail, "prompt", -1)
    own_rows = queries[0, 0]
    pair_count = lax.axis_size(("zg", "zl"))
    partner_rows = lax.ppermute(own_rows, ("zg", "zl"), [(k, pair_count - 1 - k) for k in range(pair_count)])

    def by_head(block):
        return block[0].reshape(block_len, 2, KVH, HEAD_SIZE).transpose(2, 1, 0, 3).reshape(KVH, 2 * block_len, HEAD_SIZE)

    def query_groups(rows):
        return rows.reshape(step_count, KVH, GROUP, HEAD_SIZE).transpose(1, 0, 2, 3).reshape(KVH, rows_per_sample, HEAD_SIZE)

    span = 2 * block_len
    first = lax.all_to_all(
        jnp.concatenate([by_head(prefix_head), query_groups(own_rows)], axis=1), ("zl", "core"), 0, 0, tiled=True
    )
    second = lax.all_to_all(
        jnp.concatenate([by_head(moved_tail), query_groups(partner_rows)], axis=1), ("zl", "core"), 0, 0, tiled=True
    )
    partner_part = second[:, span:].reshape(team_count // 2, 2, rows_per_sample, HEAD_SIZE)[::-1]
    query_parts = jnp.stack([first[:, span:], partner_part.reshape(team_count, rows_per_sample, HEAD_SIZE)])
    query_parts = jnp.where(team == 0, query_parts, query_parts[::-1])
    query_matrix = query_parts.reshape(2 * team_count * rows_per_sample, HEAD_SIZE)

    member = jnp.arange(team_count, dtype=jnp.int32)[None, :, None]
    half = jnp.arange(2, dtype=jnp.int32)[:, None, None]
    offset = jnp.arange(block_len, dtype=jnp.int32)[None, None, :]
    prefix_half_len = block_len * team_count * 2
    positions = half * prefix_half_len + (team * team_count + member) * block_len + offset
    bias = jnp.where(positions.reshape(2, -1) < prefix_len[prompt_row], 0.0, NEG).astype(jnp.float32)
    sample_count = 2 * team_count
    outgoing_parts = prefix_attention(bias, query_matrix, first, second, block_len, rows_per_sample)
    returned = lax.all_to_all(outgoing_parts, ("zg", "zl", "core"), 0, 0, tiled=True)
    returned = returned.reshape(2, KVH, rows_per_sample + 2, HEAD_SIZE)
    lane_offset = (lax.axis_index(("zg", "zl", "core")) % (ROW_BLOCK // rows_per_sample)) * rows_per_sample

    def unpack(parts):
        numer = parts[:, :rows_per_sample].reshape(KVH, step_count, GROUP, HEAD_SIZE)
        numer = numer.transpose(1, 0, 2, 3).reshape(step_count, QH, HEAD_SIZE)
        maxi = lax.dynamic_slice_in_dim(parts[:, rows_per_sample], lane_offset, rows_per_sample, axis=1)
        maxi = maxi.reshape(KVH, step_count, GROUP)
        maxi = maxi.transpose(1, 0, 2).reshape(step_count, QH)
        tot = lax.dynamic_slice_in_dim(parts[:, rows_per_sample + 1], lane_offset, rows_per_sample, axis=1)
        tot = tot.reshape(KVH, step_count, GROUP)
        tot = tot.transpose(1, 0, 2).reshape(step_count, QH)
        return numer, maxi, tot

    first_numer, first_max, first_tot = unpack(returned[0])
    second_numer, second_max, second_tot = unpack(returned[1])
    near_numer, near_max, near_tot = suffix_terms(own_rows, suffix_kv[0, 0], new_kv[0, 0], suffix_len[0, 0])

    top = jnp.maximum(jnp.maximum(first_max, second_max), near_max)
    first_scale = jnp.exp(first_max - top)
    second_scale = jnp.exp(second_max - top)
    near_scale = jnp.exp(near_max - top)
    numer = (
        first_numer * first_scale[..., None]
        + second_numer * second_scale[..., None]
        + near_numer * near_scale[..., None]
    )
    total = first_tot * first_scale + second_tot * second_scale + near_tot * near_scale
    attended = (numer / total[..., None]).astype(jnp.bfloat16)
    return attended.reshape(queries.shape)


def solution(mesh):
    prompts, samples = mesh.devices.shape
    teams = 2
    team_mesh = jax.sharding.Mesh(
        mesh.devices.reshape(prompts, teams, samples // (2 * teams), 2), ("prompt", "zg", "zl", "core")
    )
    spread = ("zg", "zl", "core")
    in_specs = (
        P("prompt", spread, None, None),
        P("prompt", spread, None, None, None),
        P("prompt", spread, None, None, None),
        P("prompt", spread),
        P("prompt", spread, None, None),
        P("prompt", spread, None, None),
        P(),
    )
    out_specs = P("prompt", spread, None, None)
    return jax.shard_map(
        per_device, mesh=team_mesh, in_specs=in_specs, out_specs=out_specs, check_vma=False
    )
```

```python
import functools

import jax
import jax.numpy as jnp
from jax import lax
from jax.experimental import pallas as pl
from jax.sharding import PartitionSpec as P

QH = 64
KVH = 8
HEAD_SIZE = 128
GROUP = QH // KVH


NEG = -1e30
ROW_BLOCK = 128


def prefix_kernel(block, bias_ref, query_ref, first_ref, second_ref, out_ref):
    query = query_ref[...]
    members = first_ref.shape[0]
    parts = []
    for index, source in enumerate((first_ref, second_ref)):
        keys = source[:, :block, :].reshape(members * block, HEAD_SIZE)
        values = source[:, block : 2 * block, :].reshape(members * block, HEAD_SIZE)
        scores = lax.dot_general(
            query, keys, (((1,), (1,)), ((), ())), preferred_element_type=jnp.float32
        ) * HEAD_SIZE ** (-0.5) + bias_ref[index : index + 1, :]
        parts.append((scores, values))
    maxima = jnp.maximum(
        jnp.max(parts[0][0], axis=1, keepdims=True), jnp.max(parts[1][0], axis=1, keepdims=True)
    )
    numer = None
    totals = None
    for scores, values in parts:
        weights = jnp.exp(scores - maxima)
        part_total = jnp.sum(weights, axis=1, keepdims=True)
        high = weights.astype(jnp.bfloat16)
        low = (weights - high.astype(jnp.float32)).astype(jnp.bfloat16)
        part = jnp.dot(high, values, preferred_element_type=jnp.float32) + jnp.dot(
            low, values, preferred_element_type=jnp.float32
        )
        numer = part if numer is None else numer + part
        totals = part_total if totals is None else totals + part_total
    samples, rows, width = out_ref.shape
    rows = rows - 2
    out_ref[:, :rows, :] = numer.reshape(samples, rows, width)
    max_row = jnp.transpose(jnp.broadcast_to(maxima, (ROW_BLOCK, ROW_BLOCK)))[0:1, :]
    total_row = jnp.transpose(jnp.broadcast_to(totals, (ROW_BLOCK, ROW_BLOCK)))[0:1, :]
    out_ref[:, rows : rows + 1, :] = jnp.broadcast_to(max_row[None], (samples, 1, width))
    out_ref[:, rows + 1 : rows + 2, :] = jnp.broadcast_to(total_row[None], (samples, 1, width))


def prefix_attention(bias, query_matrix, first, second, block, rows_per_sample):
    rows, width = query_matrix.shape
    span = first.shape[0] * block
    per_block = ROW_BLOCK // rows_per_sample
    return pl.pallas_call(
        functools.partial(prefix_kernel, block),
        grid=(rows // ROW_BLOCK,),
        in_specs=[
            pl.BlockSpec(bias.shape, lambda i: (0, 0)),
            pl.BlockSpec((ROW_BLOCK, width), lambda i: (i, 0)),
            pl.BlockSpec(first.shape, lambda i: (0, 0, 0)),
            pl.BlockSpec(second.shape, lambda i: (0, 0, 0)),
        ],
        out_specs=pl.BlockSpec((per_block, rows_per_sample + 2, width), lambda i: (i, 0, 0)),
        out_shape=jax.ShapeDtypeStruct((rows // rows_per_sample, rows_per_sample + 2, width), jnp.float32),
        cost_estimate=pl.CostEstimate(
            flops=3 * rows * span * width, transcendentals=rows * span // 2, bytes_accessed=2 * (rows + span) * width + 4 * rows * width
        ),
    )(bias, query_matrix, first, second)


def shifted(value, axis, steps):
    count = lax.axis_size(axis)
    pairs = [(source, (source + steps) % count) for source in range(count)]
    return lax.ppermute(value, axis, pairs)


def split_dot(weights, value_matrix, form):
    rounded = lax.reduce_precision(weights, exponent_bits=8, mantissa_bits=7)
    high = rounded.astype(jnp.bfloat16)
    low = (weights - rounded).astype(jnp.bfloat16)
    return jnp.einsum(form, high, value_matrix, preferred_element_type=jnp.float32) + jnp.einsum(
        form, low, value_matrix, preferred_element_type=jnp.float32
    )


def suffix_terms(query_rows, cache, fresh, length):
    step_count = query_rows.shape[0]
    slots = cache.shape[0]
    grouped = query_rows.reshape(step_count, KVH, GROUP, HEAD_SIZE)
    cache_keys = cache[:, 0].reshape(slots, KVH, HEAD_SIZE)
    cache_values = cache[:, 1].reshape(slots, KVH, HEAD_SIZE)
    fresh_keys = fresh[:, 0].reshape(step_count, KVH, HEAD_SIZE)
    fresh_values = fresh[:, 1].reshape(step_count, KVH, HEAD_SIZE)
    scale = HEAD_SIZE ** (-0.5)
    cache_scores = jnp.einsum("tkgd,lkd->tkgl", grouped, cache_keys, preferred_element_type=jnp.float32) * scale
    fresh_scores = jnp.einsum("tkgd,ukd->tkgu", grouped, fresh_keys, preferred_element_type=jnp.float32) * scale
    cache_live = (jnp.arange(slots, dtype=jnp.int32) < length)[None, None, None, :]
    steps_live = (
        jnp.arange(step_count, dtype=jnp.int32)[None, :] <= jnp.arange(step_count, dtype=jnp.int32)[:, None]
    )[:, None, None, :]
    cache_masked = jnp.where(cache_live, cache_scores, NEG)
    fresh_masked = jnp.where(steps_live, fresh_scores, NEG)
    maxima = jnp.maximum(jnp.max(cache_masked, axis=-1), jnp.max(fresh_masked, axis=-1))
    cache_weights = jnp.where(cache_live, jnp.exp(cache_masked - maxima[..., None]), 0.0)
    fresh_weights = jnp.where(steps_live, jnp.exp(fresh_masked - maxima[..., None]), 0.0)
    totals = jnp.sum(cache_weights, axis=-1) + jnp.sum(fresh_weights, axis=-1)
    numerator = split_dot(cache_weights, cache_values, "tkgl,lkd->ktgd") + split_dot(
        fresh_weights, fresh_values, "tkgu,ukd->ktgd"
    )
    return (
        numerator.reshape(KVH, step_count * GROUP, HEAD_SIZE),
        maxima.transpose(1, 0, 2).reshape(KVH, step_count * GROUP),
        totals.transpose(1, 0, 2).reshape(KVH, step_count * GROUP),
    )


def per_device(queries, new_kv, suffix_kv, suffix_len, prefix_head, prefix_tail, prefix_len):
    team_count = lax.axis_size(("zl", "core"))
    prompt_row = lax.axis_index("prompt")
    team = lax.axis_index("zg")
    block_len = prefix_head.shape[1]
    step_count = queries.shape[2]
    rows_per_sample = step_count * GROUP

    moved_tail = shifted(prefix_tail, "prompt", -1)
    own_rows = queries[0, 0]
    partner_rows = shifted(own_rows, "zg", 1)

    def by_head(block):
        return block[0].reshape(block_len, 2, KVH, HEAD_SIZE).transpose(2, 1, 0, 3).reshape(KVH, 2 * block_len, HEAD_SIZE)

    def query_groups(rows):
        return rows.reshape(step_count, KVH, GROUP, HEAD_SIZE).transpose(1, 0, 2, 3).reshape(KVH, rows_per_sample, HEAD_SIZE)

    span = 2 * block_len
    first = lax.all_to_all(
        jnp.concatenate([by_head(prefix_head), query_groups(own_rows)], axis=1), ("zl", "core"), 0, 0, tiled=True
    )
    second = lax.all_to_all(
        jnp.concatenate([by_head(moved_tail), query_groups(partner_rows)], axis=1), ("zl", "core"), 0, 0, tiled=True
    )
    query_parts = jnp.stack([first[:, span:], second[:, span:]])
    query_parts = jnp.where(team == 0, query_parts, query_parts[::-1])
    query_matrix = query_parts.reshape(2 * team_count * rows_per_sample, HEAD_SIZE)

    member = jnp.arange(team_count, dtype=jnp.int32)[None, :, None]
    half = jnp.arange(2, dtype=jnp.int32)[:, None, None]
    offset = jnp.arange(block_len, dtype=jnp.int32)[None, None, :]
    prefix_half_len = block_len * team_count * 2
    positions = half * prefix_half_len + (team * team_count + member) * block_len + offset
    bias = jnp.where(positions.reshape(2, -1) < prefix_len[prompt_row], 0.0, NEG).astype(jnp.float32)
    sample_count = 2 * team_count
    outgoing_parts = prefix_attention(bias, query_matrix, first, second, block_len, rows_per_sample)
    returned = lax.all_to_all(outgoing_parts, ("zg", "zl", "core"), 0, 0, tiled=True)
    returned = returned.reshape(2, KVH, rows_per_sample + 2, HEAD_SIZE)
    lane_offset = (lax.axis_index(("zg", "zl", "core")) % (ROW_BLOCK // rows_per_sample)) * rows_per_sample
    part_numer = returned[:, :, :rows_per_sample]
    part_stats = lax.dynamic_slice_in_dim(returned[:, :, rows_per_sample:], lane_offset, rows_per_sample, axis=3)
    part_max = part_stats[:, :, 0]
    part_tot = part_stats[:, :, 1]
    near_numer, near_max, near_tot = suffix_terms(own_rows, suffix_kv[0, 0], new_kv[0, 0], suffix_len[0, 0])

    top = jnp.maximum(jnp.maximum(part_max[0], part_max[1]), near_max)
    part_scale = jnp.exp(part_max - top[None])
    near_scale = jnp.exp(near_max - top)
    numer = (
        part_numer[0] * part_scale[0][..., None]
        + part_numer[1] * part_scale[1][..., None]
        + near_numer * near_scale[..., None]
    )
    total = part_tot[0] * part_scale[0] + part_tot[1] * part_scale[1] + near_tot * near_scale
    attended = (numer / total[..., None]).astype(jnp.bfloat16)
    attended = attended.reshape(KVH, step_count, GROUP, HEAD_SIZE).transpose(1, 0, 2, 3)
    return attended.reshape(queries.shape)


def solution(mesh):
    prompts, samples = mesh.devices.shape
    teams = 2
    team_mesh = jax.sharding.Mesh(
        mesh.devices.reshape(prompts, teams, samples // (2 * teams), 2), ("prompt", "zg", "zl", "core")
    )
    spread = ("zg", "zl", "core")
    in_specs = (
        P("prompt", spread, None, None),
        P("prompt", spread, None, None, None),
        P("prompt", spread, None, None, None),
        P("prompt", spread),
        P("prompt", spread, None, None),
        P("prompt", spread, None, None),
        P(),
    )
    out_specs = P("prompt", spread, None, None)
    return jax.shard_map(
        per_device, mesh=team_mesh, in_specs=in_specs, out_specs=out_specs, check_vma=False
    )
```

```python
import functools

import jax
import jax.numpy as jnp
from jax import lax
from jax.experimental import pallas as pl
from jax.sharding import PartitionSpec as P

QH = 64
KVH = 8
HEAD_SIZE = 128
GROUP = QH // KVH


NEG = -1e30
ROW_BLOCK = 128


def prefix_kernel(block, bias_ref, query_ref, first_ref, second_ref, out_ref):
    query = query_ref[...]
    members = first_ref.shape[0]
    parts = []
    for index, source in enumerate((first_ref, second_ref)):
        keys = source[:, :block, :].reshape(members * block, HEAD_SIZE)
        values = source[:, block : 2 * block, :].reshape(members * block, HEAD_SIZE)
        scores = lax.dot_general(
            query, keys, (((1,), (1,)), ((), ())), preferred_element_type=jnp.float32
        ) * HEAD_SIZE ** (-0.5) + bias_ref[index : index + 1, :]
        parts.append((scores, values))
    maxima = jnp.maximum(
        jnp.max(parts[0][0], axis=1, keepdims=True), jnp.max(parts[1][0], axis=1, keepdims=True)
    )
    numer = None
    totals = None
    for scores, values in parts:
        weights = jnp.exp(scores - maxima)
        part_total = jnp.sum(weights, axis=1, keepdims=True)
        high = weights.astype(jnp.bfloat16)
        low = (weights - high.astype(jnp.float32)).astype(jnp.bfloat16)
        part = jnp.dot(high, values, preferred_element_type=jnp.float32) + jnp.dot(
            low, values, preferred_element_type=jnp.float32
        )
        numer = part if numer is None else numer + part
        totals = part_total if totals is None else totals + part_total
    samples, rows, width = out_ref.shape
    rows = rows - 2
    out_ref[:, :rows, :] = numer.reshape(samples, rows, width)
    max_row = jnp.transpose(jnp.broadcast_to(maxima, (ROW_BLOCK, ROW_BLOCK)))[0:1, :]
    total_row = jnp.transpose(jnp.broadcast_to(totals, (ROW_BLOCK, ROW_BLOCK)))[0:1, :]
    out_ref[:, rows : rows + 1, :] = jnp.broadcast_to(max_row[None], (samples, 1, width))
    out_ref[:, rows + 1 : rows + 2, :] = jnp.broadcast_to(total_row[None], (samples, 1, width))


def prefix_attention(bias, query_matrix, first, second, block, rows_per_sample):
    rows, width = query_matrix.shape
    span = first.shape[0] * block
    per_block = ROW_BLOCK // rows_per_sample
    return pl.pallas_call(
        functools.partial(prefix_kernel, block),
        grid=(rows // ROW_BLOCK,),
        in_specs=[
            pl.BlockSpec(bias.shape, lambda i: (0, 0)),
            pl.BlockSpec((ROW_BLOCK, width), lambda i: (i, 0)),
            pl.BlockSpec(first.shape, lambda i: (0, 0, 0)),
            pl.BlockSpec(second.shape, lambda i: (0, 0, 0)),
        ],
        out_specs=pl.BlockSpec((per_block, rows_per_sample + 2, width), lambda i: (i, 0, 0)),
        out_shape=jax.ShapeDtypeStruct((rows // rows_per_sample, rows_per_sample + 2, width), jnp.float32),
        cost_estimate=pl.CostEstimate(
            flops=3 * rows * span * width, transcendentals=rows * span // 2, bytes_accessed=2 * (rows + span) * width + 4 * rows * width
        ),
    )(bias, query_matrix, first, second)


def combine_kernel(stats_ref, first_ref, second_ref, near_ref, out_ref):
    for head in range(out_ref.shape[0]):
        maxima = [stats_ref[source, 0, :, head : head + 1] for source in range(3)]
        totals = [stats_ref[source, 1, :, head : head + 1] for source in range(3)]
        top = jnp.maximum(jnp.maximum(maxima[0], maxima[1]), maxima[2])
        scales = [jnp.exp(m - top) for m in maxima]
        numer = first_ref[head] * scales[0] + second_ref[head] * scales[1] + near_ref[head] * scales[2]
        total = totals[0] * scales[0] + totals[1] * scales[1] + totals[2] * scales[2]
        out_ref[head] = (numer / total).astype(out_ref.dtype)


def shifted(value, axis, steps):
    count = lax.axis_size(axis)
    pairs = [(source, (source + steps) % count) for source in range(count)]
    return lax.ppermute(value, axis, pairs)


def split_dot(weights, value_matrix, form):
    rounded = lax.reduce_precision(weights, exponent_bits=8, mantissa_bits=7)
    high = rounded.astype(jnp.bfloat16)
    low = (weights - rounded).astype(jnp.bfloat16)
    return jnp.einsum(form, high, value_matrix, preferred_element_type=jnp.float32) + jnp.einsum(
        form, low, value_matrix, preferred_element_type=jnp.float32
    )


def suffix_terms(query_rows, cache, fresh, length):
    step_count = query_rows.shape[0]
    slots = cache.shape[0]
    grouped = query_rows.reshape(step_count, KVH, GROUP, HEAD_SIZE)
    cache_keys = cache[:, 0].reshape(slots, KVH, HEAD_SIZE)
    cache_values = cache[:, 1].reshape(slots, KVH, HEAD_SIZE)
    fresh_keys = fresh[:, 0].reshape(step_count, KVH, HEAD_SIZE)
    fresh_values = fresh[:, 1].reshape(step_count, KVH, HEAD_SIZE)
    scale = HEAD_SIZE ** (-0.5)
    cache_scores = jnp.einsum("tkgd,lkd->tkgl", grouped, cache_keys, preferred_element_type=jnp.float32) * scale
    fresh_scores = jnp.einsum("tkgd,ukd->tkgu", grouped, fresh_keys, preferred_element_type=jnp.float32) * scale
    cache_live = (jnp.arange(slots, dtype=jnp.int32) < length)[None, None, None, :]
    steps_live = (
        jnp.arange(step_count, dtype=jnp.int32)[None, :] <= jnp.arange(step_count, dtype=jnp.int32)[:, None]
    )[:, None, None, :]
    cache_masked = jnp.where(cache_live, cache_scores, NEG)
    fresh_masked = jnp.where(steps_live, fresh_scores, NEG)
    maxima = jnp.maximum(jnp.max(cache_masked, axis=-1), jnp.max(fresh_masked, axis=-1))
    cache_weights = jnp.where(cache_live, jnp.exp(cache_masked - maxima[..., None]), 0.0)
    fresh_weights = jnp.where(steps_live, jnp.exp(fresh_masked - maxima[..., None]), 0.0)
    totals = jnp.sum(cache_weights, axis=-1) + jnp.sum(fresh_weights, axis=-1)
    numerator = split_dot(cache_weights, cache_values, "tkgl,lkd->ktgd") + split_dot(
        fresh_weights, fresh_values, "tkgu,ukd->ktgd"
    )
    return (
        numerator.reshape(KVH, step_count * GROUP, HEAD_SIZE),
        maxima.transpose(1, 0, 2).reshape(KVH, step_count * GROUP),
        totals.transpose(1, 0, 2).reshape(KVH, step_count * GROUP),
    )


def per_device(queries, new_kv, suffix_kv, suffix_len, prefix_head, prefix_tail, prefix_len):
    team_count = lax.axis_size(("zl", "core"))
    prompt_row = lax.axis_index("prompt")
    team = lax.axis_index("zg")
    block_len = prefix_head.shape[1]
    step_count = queries.shape[2]
    rows_per_sample = step_count * GROUP

    moved_tail = shifted(prefix_tail, "prompt", -1)
    own_rows = queries[0, 0]
    partner_rows = shifted(own_rows, "zg", 1)

    def by_head(block):
        return block[0].reshape(block_len, 2, KVH, HEAD_SIZE).transpose(2, 1, 0, 3).reshape(KVH, 2 * block_len, HEAD_SIZE)

    def query_groups(rows):
        return rows.reshape(step_count, KVH, GROUP, HEAD_SIZE).transpose(1, 0, 2, 3).reshape(KVH, rows_per_sample, HEAD_SIZE)

    span = 2 * block_len
    first = lax.all_to_all(
        jnp.concatenate([by_head(prefix_head), query_groups(own_rows)], axis=1), ("zl", "core"), 0, 0, tiled=True
    )
    second = lax.all_to_all(
        jnp.concatenate([by_head(moved_tail), query_groups(partner_rows)], axis=1), ("zl", "core"), 0, 0, tiled=True
    )
    query_parts = jnp.stack([first[:, span:], second[:, span:]])
    query_parts = jnp.where(team == 0, query_parts, query_parts[::-1])
    query_matrix = query_parts.reshape(2 * team_count * rows_per_sample, HEAD_SIZE)

    member = jnp.arange(team_count, dtype=jnp.int32)[None, :, None]
    half = jnp.arange(2, dtype=jnp.int32)[:, None, None]
    offset = jnp.arange(block_len, dtype=jnp.int32)[None, None, :]
    prefix_half_len = block_len * team_count * 2
    positions = half * prefix_half_len + (team * team_count + member) * block_len + offset
    bias = jnp.where(positions.reshape(2, -1) < prefix_len[prompt_row], 0.0, NEG).astype(jnp.float32)
    sample_count = 2 * team_count
    outgoing_parts = prefix_attention(bias, query_matrix, first, second, block_len, rows_per_sample)
    returned = lax.all_to_all(outgoing_parts, ("zg", "zl", "core"), 0, 0, tiled=True)
    returned = returned.reshape(2, KVH, rows_per_sample + 2, HEAD_SIZE)
    lane_offset = (lax.axis_index(("zg", "zl", "core")) % (ROW_BLOCK // rows_per_sample)) * rows_per_sample
    part_numer = returned[:, :, :rows_per_sample]
    part_stats = lax.dynamic_slice_in_dim(returned[:, :, rows_per_sample:], lane_offset, rows_per_sample, axis=3)
    part_max = part_stats[:, :, 0]
    part_tot = part_stats[:, :, 1]
    near_numer, near_max, near_tot = suffix_terms(own_rows, suffix_kv[0, 0], new_kv[0, 0], suffix_len[0, 0])

    stats = jnp.stack(
        [
            jnp.stack([part_max[0], part_tot[0]]),
            jnp.stack([part_max[1], part_tot[1]]),
            jnp.stack([near_max, near_tot]),
        ]
    ).transpose(0, 1, 3, 2)
    attended = pl.pallas_call(
        combine_kernel,
        out_shape=jax.ShapeDtypeStruct((KVH, rows_per_sample, HEAD_SIZE), jnp.bfloat16),
    )(stats, part_numer[0], part_numer[1], near_numer)
    attended = attended.reshape(KVH, step_count, GROUP, HEAD_SIZE).transpose(1, 0, 2, 3)
    return attended.reshape(queries.shape)


def solution(mesh):
    prompts, samples = mesh.devices.shape
    teams = 2
    team_mesh = jax.sharding.Mesh(
        mesh.devices.reshape(prompts, teams, samples // (2 * teams), 2), ("prompt", "zg", "zl", "core")
    )
    spread = ("zg", "zl", "core")
    in_specs = (
        P("prompt", spread, None, None),
        P("prompt", spread, None, None, None),
        P("prompt", spread, None, None, None),
        P("prompt", spread),
        P("prompt", spread, None, None),
        P("prompt", spread, None, None),
        P(),
    )
    out_specs = P("prompt", spread, None, None)
    return jax.shard_map(
        per_device, mesh=team_mesh, in_specs=in_specs, out_specs=out_specs, check_vma=False
    )
```

```python
import functools

import jax
import jax.numpy as jnp
from jax import lax
from jax.experimental import pallas as pl
from jax.sharding import PartitionSpec as P

QH = 64
KVH = 8
HEAD_SIZE = 128
GROUP = QH // KVH


NEG = -1e30
ROW_BLOCK = 128


def prefix_kernel(block, bias_ref, query_ref, first_ref, second_ref, out_ref):
    query = query_ref[...]
    members = first_ref.shape[0]
    parts = []
    for index, source in enumerate((first_ref, second_ref)):
        keys = source[:, :block, :].reshape(members * block, HEAD_SIZE)
        values = source[:, block : 2 * block, :].reshape(members * block, HEAD_SIZE)
        scores = lax.dot_general(
            query, keys, (((1,), (1,)), ((), ())), preferred_element_type=jnp.float32
        ) * HEAD_SIZE ** (-0.5) + bias_ref[index : index + 1, :]
        parts.append((scores, values))
    maxima = jnp.maximum(
        jnp.max(parts[0][0], axis=1, keepdims=True), jnp.max(parts[1][0], axis=1, keepdims=True)
    )
    numer = None
    totals = None
    for scores, values in parts:
        weights = jnp.exp(scores - maxima)
        part_total = jnp.sum(weights, axis=1, keepdims=True)
        high = weights.astype(jnp.bfloat16)
        low = (weights - high.astype(jnp.float32)).astype(jnp.bfloat16)
        part = jnp.dot(high, values, preferred_element_type=jnp.float32) + jnp.dot(
            low, values, preferred_element_type=jnp.float32
        )
        numer = part if numer is None else numer + part
        totals = part_total if totals is None else totals + part_total
    samples, rows, width = out_ref.shape
    rows = rows - 2
    out_ref[:, :rows, :] = numer.reshape(samples, rows, width)
    max_row = jnp.transpose(jnp.broadcast_to(maxima, (ROW_BLOCK, ROW_BLOCK)))[0:1, :]
    total_row = jnp.transpose(jnp.broadcast_to(totals, (ROW_BLOCK, ROW_BLOCK)))[0:1, :]
    out_ref[:, rows : rows + 1, :] = jnp.broadcast_to(max_row[None], (samples, 1, width))
    out_ref[:, rows + 1 : rows + 2, :] = jnp.broadcast_to(total_row[None], (samples, 1, width))


def prefix_attention(bias, query_matrix, first, second, block, rows_per_sample):
    rows, width = query_matrix.shape
    span = first.shape[0] * block
    per_block = ROW_BLOCK // rows_per_sample
    return pl.pallas_call(
        functools.partial(prefix_kernel, block),
        grid=(rows // ROW_BLOCK,),
        in_specs=[
            pl.BlockSpec(bias.shape, lambda i: (0, 0)),
            pl.BlockSpec((ROW_BLOCK, width), lambda i: (i, 0)),
            pl.BlockSpec(first.shape, lambda i: (0, 0, 0)),
            pl.BlockSpec(second.shape, lambda i: (0, 0, 0)),
        ],
        out_specs=pl.BlockSpec((per_block, rows_per_sample + 2, width), lambda i: (i, 0, 0)),
        out_shape=jax.ShapeDtypeStruct((rows // rows_per_sample, rows_per_sample + 2, width), jnp.float32),
        cost_estimate=pl.CostEstimate(
            flops=3 * rows * span * width, transcendentals=rows * span // 2, bytes_accessed=2 * (rows + span) * width + 4 * rows * width
        ),
    )(bias, query_matrix, first, second)


def shifted(value, axis, steps):
    count = lax.axis_size(axis)
    pairs = [(source, (source + steps) % count) for source in range(count)]
    return lax.ppermute(value, axis, pairs)


def split_dot(weights, value_matrix, form):
    rounded = lax.reduce_precision(weights, exponent_bits=8, mantissa_bits=7)
    high = rounded.astype(jnp.bfloat16)
    low = (weights - rounded).astype(jnp.bfloat16)
    return jnp.einsum(form, high, value_matrix, preferred_element_type=jnp.float32) + jnp.einsum(
        form, low, value_matrix, preferred_element_type=jnp.float32
    )


def suffix_terms(query_rows, cache, fresh, length):
    step_count = query_rows.shape[0]
    slots = cache.shape[0]
    grouped = query_rows.reshape(step_count, KVH, GROUP, HEAD_SIZE)
    cache_keys = cache[:, 0].reshape(slots, KVH, HEAD_SIZE)
    cache_values = cache[:, 1].reshape(slots, KVH, HEAD_SIZE)
    fresh_keys = fresh[:, 0].reshape(step_count, KVH, HEAD_SIZE)
    fresh_values = fresh[:, 1].reshape(step_count, KVH, HEAD_SIZE)
    scale = HEAD_SIZE ** (-0.5)
    cache_scores = jnp.einsum("tkgd,lkd->tkgl", grouped, cache_keys, preferred_element_type=jnp.float32) * scale
    fresh_scores = jnp.einsum("tkgd,ukd->tkgu", grouped, fresh_keys, preferred_element_type=jnp.float32) * scale
    cache_live = (jnp.arange(slots, dtype=jnp.int32) < length)[None, None, None, :]
    steps_live = (
        jnp.arange(step_count, dtype=jnp.int32)[None, :] <= jnp.arange(step_count, dtype=jnp.int32)[:, None]
    )[:, None, None, :]
    cache_masked = jnp.where(cache_live, cache_scores, NEG)
    fresh_masked = jnp.where(steps_live, fresh_scores, NEG)
    maxima = jnp.maximum(jnp.max(cache_masked, axis=-1), jnp.max(fresh_masked, axis=-1))
    cache_weights = jnp.where(cache_live, jnp.exp(cache_masked - maxima[..., None]), 0.0)
    fresh_weights = jnp.where(steps_live, jnp.exp(fresh_masked - maxima[..., None]), 0.0)
    totals = jnp.sum(cache_weights, axis=-1) + jnp.sum(fresh_weights, axis=-1)
    numerator = split_dot(cache_weights, cache_values, "tkgl,lkd->tkgd") + split_dot(
        fresh_weights, fresh_values, "tkgu,ukd->tkgd"
    )
    return (
        numerator.reshape(step_count, QH, HEAD_SIZE),
        maxima.reshape(step_count, QH),
        totals.reshape(step_count, QH),
    )


def per_device(queries, new_kv, suffix_kv, suffix_len, prefix_head, prefix_tail, prefix_len):
    team_count = lax.axis_size(("zl", "core"))
    prompt_row = lax.axis_index("prompt")
    team = lax.axis_index("zg")
    block_len = prefix_head.shape[1]
    step_count = queries.shape[2]
    rows_per_sample = step_count * GROUP

    moved_tail = shifted(prefix_tail, "prompt", -1)
    own_rows = queries[0, 0]
    partner_rows = shifted(own_rows, "zg", 1)

    def by_head(block):
        return block[0].reshape(block_len, 2, KVH, HEAD_SIZE).transpose(2, 1, 0, 3).reshape(KVH, 2 * block_len, HEAD_SIZE)

    def query_groups(rows):
        return rows.reshape(step_count, KVH, GROUP, HEAD_SIZE).transpose(1, 0, 2, 3).reshape(KVH, rows_per_sample, HEAD_SIZE)

    span = 2 * block_len
    first = lax.all_to_all(by_head(prefix_head), ("zl", "core"), 0, 0, tiled=True)
    second = lax.all_to_all(
        jnp.concatenate([by_head(moved_tail), query_groups(own_rows), query_groups(partner_rows)], axis=1),
        ("zl", "core"),
        0,
        0,
        tiled=True,
    )
    query_parts = jnp.stack([second[:, span : span + rows_per_sample], second[:, span + rows_per_sample :]])
    query_parts = jnp.where(team == 0, query_parts, query_parts[::-1])
    query_matrix = query_parts.reshape(2 * team_count * rows_per_sample, HEAD_SIZE)

    member = jnp.arange(team_count, dtype=jnp.int32)[None, :, None]
    half = jnp.arange(2, dtype=jnp.int32)[:, None, None]
    offset = jnp.arange(block_len, dtype=jnp.int32)[None, None, :]
    prefix_half_len = block_len * team_count * 2
    positions = half * prefix_half_len + (team * team_count + member) * block_len + offset
    bias = jnp.where(positions.reshape(2, -1) < prefix_len[prompt_row], 0.0, NEG).astype(jnp.float32)
    sample_count = 2 * team_count
    outgoing_parts = prefix_attention(bias, query_matrix, first, second, block_len, rows_per_sample)
    returned = lax.all_to_all(outgoing_parts, ("zg", "zl", "core"), 0, 0, tiled=True)
    returned = returned.reshape(2, KVH, rows_per_sample + 2, HEAD_SIZE)
    lane_offset = (lax.axis_index(("zg", "zl", "core")) % (ROW_BLOCK // rows_per_sample)) * rows_per_sample

    def unpack(parts):
        numer = parts[:, :rows_per_sample].reshape(KVH, step_count, GROUP, HEAD_SIZE)
        numer = numer.transpose(1, 0, 2, 3).reshape(step_count, QH, HEAD_SIZE)
        maxi = lax.dynamic_slice_in_dim(parts[:, rows_per_sample], lane_offset, rows_per_sample, axis=1)
        maxi = maxi.reshape(KVH, step_count, GROUP)
        maxi = maxi.transpose(1, 0, 2).reshape(step_count, QH)
        tot = lax.dynamic_slice_in_dim(parts[:, rows_per_sample + 1], lane_offset, rows_per_sample, axis=1)
        tot = tot.reshape(KVH, step_count, GROUP)
        tot = tot.transpose(1, 0, 2).reshape(step_count, QH)
        return numer, maxi, tot

    first_numer, first_max, first_tot = unpack(returned[0])
    second_numer, second_max, second_tot = unpack(returned[1])
    near_numer, near_max, near_tot = suffix_terms(own_rows, suffix_kv[0, 0], new_kv[0, 0], suffix_len[0, 0])

    top = jnp.maximum(jnp.maximum(first_max, second_max), near_max)
    first_scale = jnp.exp(first_max - top)
    second_scale = jnp.exp(second_max - top)
    near_scale = jnp.exp(near_max - top)
    numer = (
        first_numer * first_scale[..., None]
        + second_numer * second_scale[..., None]
        + near_numer * near_scale[..., None]
    )
    total = first_tot * first_scale + second_tot * second_scale + near_tot * near_scale
    attended = (numer / total[..., None]).astype(jnp.bfloat16)
    return attended.reshape(queries.shape)


def solution(mesh):
    prompts, samples = mesh.devices.shape
    teams = 2
    team_mesh = jax.sharding.Mesh(
        mesh.devices.reshape(prompts, teams, samples // (2 * teams), 2), ("prompt", "zg", "zl", "core")
    )
    spread = ("zg", "zl", "core")
    in_specs = (
        P("prompt", spread, None, None),
        P("prompt", spread, None, None, None),
        P("prompt", spread, None, None, None),
        P("prompt", spread),
        P("prompt", spread, None, None),
        P("prompt", spread, None, None),
        P(),
    )
    out_specs = P("prompt", spread, None, None)
    return jax.shard_map(
        per_device, mesh=team_mesh, in_specs=in_specs, out_specs=out_specs, check_vma=False
    )
```
